512 devices in a mesh: ctx: 64 (over z, y), section: 2 (over x_hi), dp: 4 (over x_lo, core).
Axes of the slice: x: 4 (x_hi: 2, x_lo: 2; x = x_hi * 2 + x_lo), y: 8, z: 8, core: 2. Of those that a mesh axis runs over, the one named last changes fastest.
Arguments:
- query_vectors: bfloat16 [4, 8192, 1792], P('dp', 'ctx', 'section'), may hold values from -16 to 16
- key_vectors: bfloat16 [4, 8192, 256], P('dp', 'ctx', 'section'), may hold values from -16 to 16
- value_vectors: bfloat16 [4, 8192, 256], P('dp', 'ctx', 'section'), may hold values from -6 to 6
- grad_output: bfloat16 [4, 8192, 1792], P('dp', 'ctx', 'section'), may hold values from -24 to 24
- output_dots: float32 [4, 14, 8192], P('dp', 'section', 'ctx'), may hold values from -12 to 12
- frame_ids: int32 [4, 8192], P('dp'), may hold values from 0 to 63, never falling along the last dimension, each value on 1 to 256 neighbouring positions
- visual_rows: int32 [4, 64, 32], P('dp', 'ctx'), may hold values from 0 to 127, as said below
- shuffle_source: int32 [4, 128, 64], P('dp', ('ctx', 'section')), may hold values from 0 to 63, each once within a row
- qkv_weight: bfloat16 [2304, 3584], P(None, ('section', 'dp')), may hold values from -0.125 to 0.125
- projector_weight: bfloat16 [3584, 2560], P(('section', 'dp')), may hold values from -0.09375 to 0.09375
Outputs:
- grad_keys: bfloat16 [4, 8192, 256], P('dp', 'ctx', 'section')
- grad_values: bfloat16 [4, 8192, 256], P('dp', 'ctx', 'section')
- patch_grads: bfloat16 [4, 8192, 640], P('dp', ('ctx', 'section'))
The draws below stay inside these ranges and needn't reach their ends.
Inputs may be any that keep to these rules, and one draw needn't show every extreme that they name: `frame_ids`: frame numbers never fall along a sequence; a frame holds 1 to 256 tokens. `visual_rows`: each block of 128 tokens lists 32 distinct positions in increasing order. `shuffle_source`: each row is a permutation.
All inputs are finite; a program needn't handle non-finite values.
Results may differ from the reference program's by a relative error of at most 0.014.
Values may be sent and summed in bfloat16 or wider, within the bound.
No kernel may reach another device: no remote copies, remote signals or barrier semaphores. Data moves between devices by JAX's collectives and lax.ppermute only.
A program may use at most 128 MiB of HBM per device.

```python
import math
import jax
import jax.numpy as jnp
import numpy as np
from jax import lax

D = 3584
HEAD_DIM = 128
GROUP = 7
KV_HEADS = 2
Q_HEADS = 14
SIG_CHAN = 640
TOK_DEV = 128
VIS_DEV = 32
SEQ_LEN = 8192
SEQUENCES = 4
FRAME_MAX = 256
FRAME_COUNT = 64
N_CTX = 64


def draw_query_vectors(key, part):
    fresh = jax.random.fold_in(key, 1)
    shape_all = (SEQUENCES, SEQ_LEN, KV_HEADS, GROUP, HEAD_DIM)
    drawn = jnp.clip(1.4 * jax.random.normal(fresh, shape_all, jnp.float32), -8.0, 8.0)
    return drawn.reshape(SEQUENCES, SEQ_LEN, KV_HEADS * GROUP * HEAD_DIM).astype(jnp.bfloat16)


def draw_key_vectors(key, part):
    fresh = jax.random.fold_in(key, 2)
    shape_all = (SEQUENCES, SEQ_LEN, KV_HEADS, HEAD_DIM)
    drawn = jnp.clip(1.4 * jax.random.normal(fresh, shape_all, jnp.float32), -8.0, 8.0)
    return drawn.reshape(SEQUENCES, SEQ_LEN, KV_HEADS * HEAD_DIM).astype(jnp.bfloat16)


def draw_visual_rows(key, part):
    block_total = SEQ_LEN // TOK_DEV
    ranks = jax.random.randint(jax.random.fold_in(key, 3), (SEQUENCES, block_total, TOK_DEV), 0, 1 << 20)
    distinct = ranks * TOK_DEV + jnp.arange(TOK_DEV, dtype=jnp.int32)
    order = jnp.argsort(distinct, axis=-1)[:, :, :VIS_DEV]
    return jnp.sort(order, axis=-1).astype(jnp.int32)


def levels(rng, shape, shards, smallest, top_value):
    level = 1.0
    for axis_at, blocks in shards:
        steps = jax.random.uniform(jax.random.fold_in(jax.random.fold_in(rng, 6), axis_at), (blocks,), jnp.float32, smallest / len(shards), top_value / len(shards))
        level = level * jnp.repeat(jnp.exp(steps), shape[axis_at] // blocks).reshape((-1,) + (1,) * (len(shape) - 1 - axis_at))
    return level


def length_profile(number_of, total, most, lean):
    portions = [(1 << 20) // math.isqrt(standing ** lean) + 1 for standing in range(2, number_of + 1)]
    surplus, holding = total - most - (number_of - 1), [1] * (number_of - 1)
    while surplus > 0:
        movable = [i for i in range(number_of - 1) if holding[i] < most]
        whole, left = sum([portions[i] for i in movable]), surplus
        for i in movable:
            more = min(most - holding[i], max(1, left * portions[i] // whole), surplus)
            holding[i] = holding[i] + more
            surplus = surplus - more
    return np.array([most] + holding)


def uneven_parts(key, amount, total, most, lean):
    if amount == 2:
        one = jax.random.randint(key, (), max(1, total - most), min(most, total - 1) + 1)
        return jnp.stack([one, total - one])
    sizes = jnp.asarray(length_profile(amount, total, most, lean), jnp.int32)
    twos = (amount - 1) // 2
    donor, taker = sizes[1:1 + 2 * twos:2], sizes[2:2 + 2 * twos:2]
    slack = jnp.minimum(donor - 1, most - taker)
    passed = jax.random.randint(jax.random.fold_in(key, 1), (twos,), 0, 1 << 20) % (slack + 1)
    sizes = sizes.at[1:1 + 2 * twos:2].set(donor - passed).at[2:2 + 2 * twos:2].set(taker + passed)
    return sizes[jax.random.permutation(jax.random.fold_in(key, 2), amount)]


def noise(rng, shape, spread, bound, cuts=(), kind=jnp.bfloat16):
    loudness = levels(rng, shape, cuts, -0.22, 0.18) if cuts else 1.0
    values = jax.random.normal(rng, shape, jnp.float32) * spread * loudness
    return jnp.minimum(jnp.maximum(values, -bound), bound).astype(kind)


def setup_inputs(seed: int = 0) -> dict:
    key_list = jax.random.split(jax.random.key(seed), 11)
    query_vectors = draw_query_vectors(jax.random.fold_in(key_list[10], 71), 0)
    key_vectors = draw_key_vectors(jax.random.fold_in(key_list[10], 71), 0)
    value_vectors = noise(key_list[2], (SEQUENCES, SEQ_LEN, KV_HEADS * HEAD_DIM), 1.0, 6.0, ((0, 4), (1, 64), (2, 2)))
    grad_output = noise(key_list[3], (SEQUENCES, SEQ_LEN, Q_HEADS * HEAD_DIM), 4.0, 24.0, ((0, 4), (1, 64), (2, 2)))
    output_dots = noise(key_list[4], (SEQUENCES, Q_HEADS, SEQ_LEN), 2.0, 12.0, ((0, 4), (1, 2), (2, 64)), jnp.float32)
    frame_ids = jax.vmap(lambda own: jnp.searchsorted(jnp.cumsum(uneven_parts(own, FRAME_COUNT, SEQ_LEN, FRAME_MAX, 0)), jnp.arange(SEQ_LEN), side="right"))(jax.random.split(key_list[5], SEQUENCES)).reshape((SEQUENCES, SEQ_LEN)).astype(jnp.int32)
    visual_rows = draw_visual_rows(jax.random.fold_in(key_list[10], 71), 0)
    shuffle_source = jax.vmap(lambda own: jax.random.permutation(own, 2 * VIS_DEV))(jax.random.split(key_list[7], SEQUENCES * (2 * N_CTX))).reshape((SEQUENCES, 2 * N_CTX, 2 * VIS_DEV)).astype(jnp.int32)
    qkv_weight = noise(key_list[8], (KV_HEADS * (GROUP + 2) * HEAD_DIM, D), (KV_HEADS * (GROUP + 2) * HEAD_DIM) ** -0.5, 0.125, ((1, 8),))
    projector_weight = noise(key_list[9], (D, 4 * SIG_CHAN), D ** -0.5, 0.09375, ((0, 8),))
    return dict(query_vectors=query_vectors, key_vectors=key_vectors, value_vectors=value_vectors, grad_output=grad_output, output_dots=output_dots, frame_ids=frame_ids, visual_rows=visual_rows, shuffle_source=shuffle_source, qkv_weight=qkv_weight, projector_weight=projector_weight)


MASKED = -1e+30

def block_mask(frame_line, query_first, key_first, width):
    query_pos = query_first + jnp.arange(width, dtype=jnp.int32)
    key_pos = key_first + jnp.arange(width, dtype=jnp.int32)
    query_frames = lax.dynamic_slice_in_dim(frame_line, query_first, width)
    key_frames = lax.dynamic_slice_in_dim(frame_line, key_first, width)
    allowed = (key_pos[None, :] <= query_pos[:, None]) | (key_frames[None, :] == query_frames[:, None])
    return (allowed, key_frames[0] <= query_frames[width - 1])

def group_backward(query_f, key_f, value_f, grad_f, dots_f, frame_line):
    seq_total = key_f.shape[0]
    width = min(512, seq_total)
    block_count = seq_total // width
    heads_here = query_f.shape[1]
    head_size = query_f.shape[2]
    scale_factor = 1.0 / math.sqrt(head_size)

    def score_block(query_block, key_block):
        return jnp.einsum('qhd,kd->hqk', query_block, key_block, precision=lax.Precision.HIGHEST) * scale_factor

    def statistics(query_index):
        query_first = (query_index * width).astype(jnp.int32)
        query_block = lax.dynamic_slice_in_dim(query_f, query_first, width, 0)

        def visit(key_index, carried):
            key_first = (jnp.asarray(key_index).astype(jnp.int32) * width).astype(jnp.int32)
            allowed, needed = block_mask(frame_line, query_first, key_first, width)

            def update(pair_state):
                running, summed = pair_state
                key_block = lax.dynamic_slice_in_dim(key_f, key_first, width, 0)
                scores = jnp.where(allowed[None], score_block(query_block, key_block), MASKED)
                newest = jnp.maximum(running, scores.max(axis=-1))
                summed = summed * jnp.exp(running - newest) + jnp.exp(scores - newest[:, :, None]).sum(axis=-1)
                return (newest, summed)
            return lax.cond(needed, update, lambda unchanged: unchanged, carried)
        start_pair = (jnp.full((heads_here, width), MASKED, jnp.float32), jnp.zeros((heads_here, width), jnp.float32))
        running, summed = lax.fori_loop(0, block_count, visit, start_pair)
        return running + jnp.log(summed)
    lse_all = lax.map(statistics, jnp.arange(block_count, dtype=jnp.int32))

    def query_step(carried, query_index):
        grad_k, grad_v = carried
        query_first = (query_index * width).astype(jnp.int32)
        query_block = lax.dynamic_slice_in_dim(query_f, query_first, width, 0)
        grad_block = lax.dynamic_slice_in_dim(grad_f, query_first, width, 0)
        dots_block = lax.dynamic_slice_in_dim(dots_f, query_first, width, 1)
        lse_block = lse_all[query_index]

        def visit(key_index, state_now):
            key_first = (jnp.asarray(key_index).astype(jnp.int32) * width).astype(jnp.int32)
            allowed, needed = block_mask(frame_line, query_first, key_first, width)

            def update(inner_state):
                grad_q, grad_keys_now, grad_values_now = inner_state
                key_block = lax.dynamic_slice_in_dim(key_f, key_first, width, 0)
                value_block = lax.dynamic_slice_in_dim(value_f, key_first, width, 0)
                scores = score_block(query_block, key_block)
                probability = jnp.exp(jnp.where(allowed[None], scores - lse_block[:, :, None], MASKED))
                probs_low = lax.optimization_barrier(probability.astype(jnp.bfloat16)).astype(jnp.float32)
                grad_probs = jnp.einsum('qhd,kd->hqk', grad_block, value_block, precision=lax.Precision.HIGHEST)
                grad_scores = lax.optimization_barrier((probability * (grad_probs - dots_block[:, :, None])).astype(jnp.bfloat16)).astype(jnp.float32)
                grad_q = grad_q + jnp.einsum('hqk,kd->qhd', grad_scores, key_block, precision=lax.Precision.HIGHEST) * scale_factor
                key_term = jnp.einsum('hqk,qhd->kd', grad_scores, query_block, precision=lax.Precision.HIGHEST) * scale_factor
                value_term = jnp.einsum('hqk,qhd->kd', probs_low, grad_block, precision=lax.Precision.HIGHEST)
                grad_keys_now = lax.dynamic_update_slice_in_dim(grad_keys_now, lax.dynamic_slice_in_dim(grad_keys_now, key_first, width, 0) + key_term, key_first, 0)
                grad_values_now = lax.dynamic_update_slice_in_dim(grad_values_now, lax.dynamic_slice_in_dim(grad_values_now, key_first, width, 0) + value_term, key_first, 0)
                return (grad_q, grad_keys_now, grad_values_now)
            return lax.cond(needed, update, lambda unchanged: unchanged, state_now)
        zero_query = jnp.zeros((width, heads_here, head_size), jnp.float32)
        grad_q, grad_k, grad_v = lax.fori_loop(0, block_count, visit, (zero_query, grad_k, grad_v))
        return ((grad_k, grad_v), grad_q)
    zero_keys = jnp.zeros((seq_total, head_size), jnp.float32)
    (grad_k, grad_v), grad_q = lax.scan(query_step, (zero_keys, zero_keys), jnp.arange(block_count, dtype=jnp.int32))
    return (grad_q.reshape(seq_total, heads_here, head_size), grad_k, grad_v)

def reference(query_vectors, key_vectors, value_vectors, grad_output, output_dots, frame_ids, visual_rows, shuffle_source, qkv_weight, projector_weight):
    query_all = query_vectors.astype(jnp.float32).reshape(SEQUENCES, SEQ_LEN, KV_HEADS, GROUP, HEAD_DIM)
    grad_all = grad_output.astype(jnp.float32).reshape(SEQUENCES, SEQ_LEN, KV_HEADS, GROUP, HEAD_DIM)
    key_all = key_vectors.astype(jnp.float32).reshape(SEQUENCES, SEQ_LEN, KV_HEADS, HEAD_DIM)
    value_all = value_vectors.astype(jnp.float32).reshape(SEQUENCES, SEQ_LEN, KV_HEADS, HEAD_DIM)
    dots_all = output_dots.reshape(SEQUENCES, KV_HEADS, GROUP, SEQ_LEN)
    key_grads = []
    value_grads = []
    patch_list = []
    for seq_index in range(SEQUENCES):
        query_parts = []
        key_parts = []
        value_parts = []
        for head_group in range(KV_HEADS):
            grad_q, grad_k, grad_v = group_backward(query_all[seq_index, :, head_group], key_all[seq_index, :, head_group], value_all[seq_index, :, head_group], grad_all[seq_index, :, head_group], dots_all[seq_index, head_group], frame_ids[seq_index])
            query_parts.append(grad_q.astype(jnp.bfloat16).reshape(SEQ_LEN, GROUP * HEAD_DIM))
            key_parts.append(grad_k.astype(jnp.bfloat16))
            value_parts.append(grad_v.astype(jnp.bfloat16))
        positions = (jnp.arange(N_CTX, dtype=jnp.int32)[:, None] * TOK_DEV + visual_rows[seq_index].astype(jnp.int32)).reshape(-1)
        picked = jnp.concatenate([jnp.concatenate([query_parts[head_group][positions], key_parts[head_group][positions], value_parts[head_group][positions]], axis=1) for head_group in range(KV_HEADS)], axis=1)
        visual_grad = jnp.dot(picked, qkv_weight, preferred_element_type=jnp.float32).astype(jnp.bfloat16)
        shuffled = jnp.dot(visual_grad, projector_weight, preferred_element_type=jnp.float32)
        slot_rows = shuffled.reshape(N_CTX * 2, VIS_DEV // 2 * 4, SIG_CHAN)
        patches = jnp.take_along_axis(slot_rows, shuffle_source[seq_index][:, :, None], axis=1)
        patch_list.append(patches.reshape(N_CTX * 4 * VIS_DEV, SIG_CHAN).astype(jnp.bfloat16))
        key_grads.append(jnp.stack(key_parts, axis=1).reshape(SEQ_LEN, KV_HEADS * HEAD_DIM))
        value_grads.append(jnp.stack(value_parts, axis=1).reshape(SEQ_LEN, KV_HEADS * HEAD_DIM))
    return (jnp.stack(key_grads), jnp.stack(value_grads), jnp.stack(patch_list))
```

```python
import math

import jax
import jax.numpy as jnp
from jax import lax
from jax.sharding import PartitionSpec as P

HEAD_DIM = 128
GROUP = 7


MASKED = -1e30


def shards(
    query_vectors,
    key_vectors,
    value_vectors,
    grad_output,
    output_dots,
    frame_ids,
    visual_rows,
    shuffle_source,
    qkv_weight,
    projector_weight,
):
    position = lax.axis_index("ctx")
    local_rows = query_vectors.shape[1]
    scale_factor = 1.0 / math.sqrt(HEAD_DIM)
    query_heads = query_vectors[0].reshape(local_rows, GROUP, HEAD_DIM)
    grad_heads = grad_output[0].reshape(local_rows, GROUP, HEAD_DIM)
    corrections = output_dots[0]
    frame_line = frame_ids[0]
    seq_total = frame_line.shape[0]
    query_first = position * local_rows
    query_pos = query_first + jnp.arange(local_rows, dtype=jnp.int32)
    query_frames = lax.dynamic_slice_in_dim(frame_line, query_first, local_rows)

    own_pair = jnp.concatenate([key_vectors[0], value_vectors[0]], axis=1)
    all_pairs = lax.all_gather(own_pair, "ctx", axis=0, tiled=True)
    key_all = all_pairs[:, :HEAD_DIM]
    value_all = all_pairs[:, HEAD_DIM:]

    key_pos = jnp.arange(seq_total, dtype=jnp.int32)
    allowed = (key_pos[None, :] <= query_pos[:, None]) | (frame_line[None, :] == query_frames[:, None])

    scores = (
        jnp.einsum("qhd,kd->hqk", query_heads, key_all, preferred_element_type=jnp.float32)
        * scale_factor
    )
    masked_scores = jnp.where(allowed[None], scores, MASKED)
    running = masked_scores.max(axis=-1)
    summed = jnp.exp(masked_scores - running[:, :, None]).sum(axis=-1)
    log_total = running + jnp.log(summed)

    probability = jnp.exp(jnp.where(allowed[None], scores - log_total[:, :, None], MASKED))
    probs_low = probability.astype(jnp.bfloat16)
    grad_probs = jnp.einsum(
        "qhd,kd->hqk", grad_heads, value_all, preferred_element_type=jnp.float32
    )
    grad_scores = (probability * (grad_probs - corrections[:, :, None])).astype(jnp.bfloat16)
    grad_query = (
        jnp.einsum("hqk,kd->qhd", grad_scores, key_all, preferred_element_type=jnp.float32)
        * scale_factor
    )
    key_part = (
        jnp.einsum("hqk,qhd->kd", grad_scores, query_heads, preferred_element_type=jnp.float32)
        * scale_factor
    )
    value_part = jnp.einsum(
        "hqk,qhd->kd", probs_low, grad_heads, preferred_element_type=jnp.float32
    )
    summed_grads = lax.psum_scatter(
        jnp.concatenate([key_part, value_part], axis=1), "ctx", scatter_dimension=0, tiled=True
    )
    grad_keys_low = summed_grads[:, :HEAD_DIM].astype(jnp.bfloat16)
    grad_values_low = summed_grads[:, HEAD_DIM:].astype(jnp.bfloat16)
    grad_query_low = grad_query.astype(jnp.bfloat16).reshape(local_rows, GROUP * HEAD_DIM)
    visual_picks = visual_rows[0, 0]
    chosen = jnp.concatenate(
        [grad_query_low[visual_picks], grad_keys_low[visual_picks], grad_values_low[visual_picks]],
        axis=1,
    )
    everyone = lax.all_gather(chosen[None], ("section", "dp"), axis=0, tiled=True)
    groups = lax.axis_size("section")
    replicas = lax.axis_size("dp")
    half_rows = visual_picks.shape[0] // 2
    width_in = chosen.shape[1]
    arranged = (
        everyone.reshape(groups, replicas, 2, half_rows, width_in)
        .transpose(2, 1, 3, 0, 4)
        .reshape(2 * replicas * half_rows, groups * width_in)
    )
    visual_grad = jnp.dot(arranged, qkv_weight, preferred_element_type=jnp.float32).astype(
        jnp.bfloat16
    )
    shuffled = lax.psum_scatter(
        jnp.dot(visual_grad, projector_weight, preferred_element_type=jnp.float32).astype(
            jnp.bfloat16
        ),
        ("section", "dp"),
        scatter_dimension=0,
        tiled=True,
    ).astype(jnp.float32)
    slot_rows = shuffled.reshape(half_rows * 4, projector_weight.shape[1] // 4)
    patches = slot_rows[shuffle_source[0, 0]].astype(jnp.bfloat16)
    return (grad_keys_low[None], grad_values_low[None], patches[None])


def solution(mesh):
    placed = (
        P("dp", "ctx", "section"),
        P("dp", "ctx", "section"),
        P("dp", "ctx", "section"),
        P("dp", "ctx", "section"),
        P("dp", "section", "ctx"),
        P("dp", None),
        P("dp", "ctx", None),
        P("dp", ("ctx", "section"), None),
        P(None, ("section", "dp")),
        P(("section", "dp"), None),
    )
    return jax.shard_map(
        shards,
        mesh=mesh,
        in_specs=placed,
        out_specs=(
            P("dp", "ctx", "section"),
            P("dp", "ctx", "section"),
            P("dp", ("ctx", "section"), None),
        ),
        check_vma=False,
    )
```

```python
import math

import jax
import jax.numpy as jnp
from jax import lax
from jax.sharding import PartitionSpec as P

HEAD_DIM = 128
GROUP = 7


MASKED = -1e30


def shards(
    query_vectors,
    key_vectors,
    value_vectors,
    grad_output,
    output_dots,
    frame_ids,
    visual_rows,
    shuffle_source,
    qkv_weight,
    projector_weight,
):
    ring_z = lax.axis_size("cz")
    ring_y = lax.axis_size("cy")
    position = lax.axis_index("cz") * ring_y + lax.axis_index("cy")
    local_rows = query_vectors.shape[1]
    scale_factor = 1.0 / math.sqrt(HEAD_DIM)
    query_heads = query_vectors[0].reshape(local_rows, GROUP, HEAD_DIM)
    grad_heads = grad_output[0].reshape(local_rows, GROUP, HEAD_DIM)
    corrections = output_dots[0]
    frame_line = frame_ids[0]
    seq_total = frame_line.shape[0]
    query_first = position * local_rows
    query_pos = query_first + jnp.arange(local_rows, dtype=jnp.int32)
    query_frames = lax.dynamic_slice_in_dim(frame_line, query_first, local_rows)

    own_pair = jnp.concatenate([key_vectors[0], value_vectors[0]], axis=1)
    all_pairs = lax.all_gather(
        lax.all_gather(own_pair, "cz", axis=0, tiled=True), "cy", axis=0, tiled=True
    )
    key_all = all_pairs[:, :HEAD_DIM]
    value_all = all_pairs[:, HEAD_DIM:]

    key_pos = (
        jnp.arange(seq_total, dtype=jnp.int32)
        .reshape(ring_z, ring_y, local_rows)
        .transpose(1, 0, 2)
        .reshape(seq_total)
    )
    key_frames = (
        frame_line.reshape(ring_z, ring_y, local_rows).transpose(1, 0, 2).reshape(seq_total)
    )
    allowed = (key_pos[None, :] <= query_pos[:, None]) | (key_frames[None, :] == query_frames[:, None])

    scores = (
        jnp.einsum("qhd,kd->hqk", query_heads, key_all, preferred_element_type=jnp.float32)
        * scale_factor
    )
    masked_scores = jnp.where(allowed[None], scores, MASKED)
    running = masked_scores.max(axis=-1)
    summed = jnp.exp(masked_scores - running[:, :, None]).sum(axis=-1)
    log_total = running + jnp.log(summed)

    probability = jnp.exp(jnp.where(allowed[None], scores - log_total[:, :, None], MASKED))
    probs_low = probability.astype(jnp.bfloat16)
    grad_probs = jnp.einsum(
        "qhd,kd->hqk", grad_heads, value_all, preferred_element_type=jnp.float32
    )
    grad_scores = (probability * (grad_probs - corrections[:, :, None])).astype(jnp.bfloat16)
    grad_query = (
        jnp.einsum("hqk,kd->qhd", grad_scores, key_all, preferred_element_type=jnp.float32)
        * scale_factor
    )
    key_part = (
        jnp.einsum("hqk,qhd->kd", grad_scores, query_heads, preferred_element_type=jnp.float32)
        * scale_factor
    )
    value_part = jnp.einsum(
        "hqk,qhd->kd", probs_low, grad_heads, preferred_element_type=jnp.float32
    )
    summed_grads = lax.psum_scatter(
        lax.psum_scatter(
            jnp.concatenate([key_part, value_part], axis=1),
            "cy",
            scatter_dimension=0,
            tiled=True,
        ),
        "cz",
        scatter_dimension=0,
        tiled=True,
    )
    grad_keys_low = summed_grads[:, :HEAD_DIM].astype(jnp.bfloat16)
    grad_values_low = summed_grads[:, HEAD_DIM:].astype(jnp.bfloat16)
    grad_query_low = grad_query.astype(jnp.bfloat16).reshape(local_rows, GROUP * HEAD_DIM)
    visual_picks = visual_rows[0, 0]
    chosen = jnp.concatenate(
        [grad_query_low[visual_picks], grad_keys_low[visual_picks], grad_values_low[visual_picks]],
        axis=1,
    )
    everyone = lax.all_gather(chosen[None], ("section", "dp"), axis=0, tiled=True)
    groups = lax.axis_size("section")
    replicas = lax.axis_size("dp")
    half_rows = visual_picks.shape[0] // 2
    width_in = chosen.shape[1]
    arranged = (
        everyone.reshape(groups, replicas, 2, half_rows, width_in)
        .transpose(2, 1, 3, 0, 4)
        .reshape(2 * replicas * half_rows, groups * width_in)
    )
    visual_grad = jnp.dot(arranged, qkv_weight, preferred_element_type=jnp.float32).astype(
        jnp.bfloat16
    )
    shuffled = lax.psum_scatter(
        jnp.dot(visual_grad, projector_weight, preferred_element_type=jnp.float32).astype(
            jnp.bfloat16
        ),
        ("section", "dp"),
        scatter_dimension=0,
        tiled=True,
    ).astype(jnp.float32)
    slot_rows = shuffled.reshape(half_rows * 4, projector_weight.shape[1] // 4)
    patches = slot_rows[shuffle_source[0, 0]].astype(jnp.bfloat16)
    return (grad_keys_low[None], grad_values_low[None], patches[None])


def solution(mesh):
    ctx_size = mesh.shape["ctx"]
    ring_y = 8 if ctx_size % 8 == 0 else 1
    split_mesh = jax.sharding.Mesh(
        mesh.devices.reshape(
            ctx_size // ring_y, ring_y, mesh.shape["section"], mesh.shape["dp"]
        ),
        ("cz", "cy", "section", "dp"),
    )
    ctx = ("cz", "cy")
    placed = (
        P("dp", ctx, "section"),
        P("dp", ctx, "section"),
        P("dp", ctx, "section"),
        P("dp", ctx, "section"),
        P("dp", "section", ctx),
        P("dp", None),
        P("dp", ctx, None),
        P("dp", ("cz", "cy", "section"), None),
        P(None, ("section", "dp")),
        P(("section", "dp"), None),
    )
    return jax.shard_map(
        shards,
        mesh=split_mesh,
        in_specs=placed,
        out_specs=(
            P("dp", ctx, "section"),
            P("dp", ctx, "section"),
            P("dp", ("cz", "cy", "section"), None),
        ),
        check_vma=False,
    )
```

```python
import math

import jax
import jax.numpy as jnp
from jax import lax
from jax.sharding import PartitionSpec as P

HEAD_DIM = 128
GROUP = 7


MASKED = -1e30


def shards(
    query_vectors,
    key_vectors,
    value_vectors,
    grad_output,
    output_dots,
    frame_ids,
    visual_rows,
    shuffle_source,
    qkv_weight,
    projector_weight,
):
    ring_z = lax.axis_size("cz")
    ring_y = lax.axis_size("cy")
    position = lax.axis_index("cz") * ring_y + lax.axis_index("cy")
    local_rows = query_vectors.shape[1]
    scale_factor = 1.0 / math.sqrt(HEAD_DIM)
    query_heads = query_vectors[0].reshape(local_rows, GROUP, HEAD_DIM)
    grad_heads = grad_output[0].reshape(local_rows, GROUP, HEAD_DIM)
    corrections = output_dots[0]
    frame_line = frame_ids[0]
    seq_total = frame_line.shape[0]
    query_first = position * local_rows
    query_pos = query_first + jnp.arange(local_rows, dtype=jnp.int32)
    query_frames = lax.dynamic_slice_in_dim(frame_line, query_first, local_rows)

    own_pair = jnp.concatenate([key_vectors[0], value_vectors[0]], axis=1)
    all_pairs = lax.all_gather(
        lax.all_gather(own_pair, "cz", axis=0, tiled=True), "cy", axis=0, tiled=True
    )
    key_all = all_pairs[:, :HEAD_DIM]
    value_all = all_pairs[:, HEAD_DIM:]

    key_pos = (
        jnp.arange(seq_total, dtype=jnp.int32)
        .reshape(ring_z, ring_y, local_rows)
        .transpose(1, 0, 2)
        .reshape(seq_total)
    )
    key_frames = (
        frame_line.reshape(ring_z, ring_y, local_rows).transpose(1, 0, 2).reshape(seq_total)
    )
    allowed = (key_pos[None, :] <= query_pos[:, None]) | (key_frames[None, :] == query_frames[:, None])

    scores = (
        jnp.einsum("qhd,kd->hqk", query_heads, key_all, preferred_element_type=jnp.float32)
        * scale_factor
    )
    masked_scores = jnp.where(allowed[None], scores, MASKED)
    running = masked_scores.max(axis=-1)
    summed = jnp.exp(masked_scores - running[:, :, None]).sum(axis=-1)
    log_total = running + jnp.log(summed)

    def chunk_grads(chunk_keys, chunk_values, chunk_allowed, chunk_scores):
        probability = jnp.exp(
            jnp.where(chunk_allowed[None], chunk_scores - log_total[:, :, None], MASKED)
        )
        probs_low = probability.astype(jnp.bfloat16)
        grad_probs = jnp.einsum(
            "qhd,kd->hqk", grad_heads, chunk_values, preferred_element_type=jnp.float32
        )
        grad_scores = (probability * (grad_probs - corrections[:, :, None])).astype(jnp.bfloat16)
        query_term = (
            jnp.einsum("hqk,kd->qhd", grad_scores, chunk_keys, preferred_element_type=jnp.float32)
            * scale_factor
        )
        key_part = (
            jnp.einsum(
                "hqk,qhd->kd", grad_scores, query_heads, preferred_element_type=jnp.float32
            )
            * scale_factor
        )
        value_part = jnp.einsum(
            "hqk,qhd->kd", probs_low, grad_heads, preferred_element_type=jnp.float32
        )
        partial = lax.psum_scatter(
            jnp.concatenate([key_part, value_part], axis=1),
            "cy",
            scatter_dimension=0,
            tiled=True,
        )
        return query_term, partial

    def chunk_of(array, lo, hi):
        lead = array.reshape((ring_y, ring_z, local_rows) + array.shape[1:])[:, lo:hi]
        return lead.reshape((ring_y * (hi - lo) * local_rows,) + array.shape[1:])

    half_z = ring_z // 2
    query_terms = []
    partials = []
    for lo, hi in ((0, half_z), (half_z, ring_z)):
        chunk_allowed = chunk_of(allowed.T, lo, hi).T
        chunk_scores = chunk_of(scores.transpose(2, 0, 1), lo, hi).transpose(1, 2, 0)
        query_term, partial = chunk_grads(
            chunk_of(key_all, lo, hi), chunk_of(value_all, lo, hi), chunk_allowed, chunk_scores
        )
        query_terms.append(query_term)
        partials.append(partial)
    grad_query = query_terms[0] + query_terms[1]
    summed_grads = lax.psum_scatter(
        jnp.concatenate(partials, axis=0), "cz", scatter_dimension=0, tiled=True
    )
    grad_keys_low = summed_grads[:, :HEAD_DIM].astype(jnp.bfloat16)
    grad_values_low = summed_grads[:, HEAD_DIM:].astype(jnp.bfloat16)
    grad_query_low = grad_query.astype(jnp.bfloat16).reshape(local_rows, GROUP * HEAD_DIM)
    visual_picks = visual_rows[0, 0]
    query_chosen = grad_query_low[visual_picks]
    pair_chosen = jnp.concatenate(
        [grad_keys_low[visual_picks], grad_values_low[visual_picks]], axis=1
    )
    everyone = jnp.concatenate(
        [
            lax.all_gather(query_chosen[None], ("section", "dp"), axis=0, tiled=True),
            lax.all_gather(pair_chosen[None], ("section", "dp"), axis=0, tiled=True),
        ],
        axis=2,
    )
    groups = lax.axis_size("section")
    replicas = lax.axis_size("dp")
    half_rows = visual_picks.shape[0] // 2
    width_in = everyone.shape[2]
    arranged = (
        everyone.reshape(groups, replicas, 2, half_rows, width_in)
        .transpose(2, 1, 3, 0, 4)
        .reshape(2 * replicas * half_rows, groups * width_in)
    )
    visual_grad = jnp.dot(arranged, qkv_weight, preferred_element_type=jnp.float32).astype(
        jnp.bfloat16
    )
    shuffled = lax.psum_scatter(
        jnp.dot(visual_grad, projector_weight, preferred_element_type=jnp.float32).astype(
            jnp.bfloat16
        ),
        ("section", "dp"),
        scatter_dimension=0,
        tiled=True,
    ).astype(jnp.float32)
    slot_rows = shuffled.reshape(half_rows * 4, projector_weight.shape[1] // 4)
    patches = slot_rows[shuffle_source[0, 0]].astype(jnp.bfloat16)
    return (grad_keys_low[None], grad_values_low[None], patches[None])


def solution(mesh):
    ctx_size = mesh.shape["ctx"]
    ring_y = 8 if ctx_size % 8 == 0 else 1
    split_mesh = jax.sharding.Mesh(
        mesh.devices.reshape(
            ctx_size // ring_y, ring_y, mesh.shape["section"], mesh.shape["dp"]
        ),
        ("cz", "cy", "section", "dp"),
    )
    ctx = ("cz", "cy")
    placed = (
        P("dp", ctx, "section"),
        P("dp", ctx, "section"),
        P("dp", ctx, "section"),
        P("dp", ctx, "section"),
        P("dp", "section", ctx),
        P("dp", None),
        P("dp", ctx, None),
        P("dp", ("cz", "cy", "section"), None),
        P(None, ("section", "dp")),
        P(("section", "dp"), None),
    )
    return jax.shard_map(
        shards,
        mesh=split_mesh,
        in_specs=placed,
        out_specs=(
            P("dp", ctx, "section"),
            P("dp", ctx, "section"),
            P("dp", ("cz", "cy", "section"), None),
        ),
        check_vma=False,
    )
```

```python
import math

import jax
import jax.numpy as jnp
from jax import lax
from jax.sharding import PartitionSpec as P

HEAD_DIM = 128
GROUP = 7


MASKED = -1e30


def shards(
    query_vectors,
    key_vectors,
    value_vectors,
    grad_output,
    output_dots,
    frame_ids,
    visual_rows,
    shuffle_source,
    qkv_weight,
    projector_weight,
):
    ring_z = lax.axis_size("cz")
    ring_y = lax.axis_size("cy")
    position = lax.axis_index("cz") * ring_y + lax.axis_index("cy")
    local_rows = query_vectors.shape[1]
    scale_factor = 1.0 / math.sqrt(HEAD_DIM)
    query_heads = query_vectors[0].reshape(local_rows, GROUP, HEAD_DIM)
    grad_heads = grad_output[0].reshape(local_rows, GROUP, HEAD_DIM)
    corrections = output_dots[0]
    frame_line = frame_ids[0]
    seq_total = frame_line.shape[0]
    query_first = position * local_rows
    query_pos = query_first + jnp.arange(local_rows, dtype=jnp.int32)
    query_frames = lax.dynamic_slice_in_dim(frame_line, query_first, local_rows)

    own_pair = jnp.concatenate([key_vectors[0], value_vectors[0]], axis=1)
    all_pairs = lax.all_gather(
        lax.all_gather(own_pair, "cz", axis=0, tiled=True), "cy", axis=0, tiled=True
    )
    key_all = all_pairs[:, :HEAD_DIM]
    value_all = all_pairs[:, HEAD_DIM:]

    key_pos = (
        jnp.arange(seq_total, dtype=jnp.int32)
        .reshape(ring_z, ring_y, local_rows)
        .transpose(1, 0, 2)
        .reshape(seq_total)
    )
    key_frames = (
        frame_line.reshape(ring_z, ring_y, local_rows).transpose(1, 0, 2).reshape(seq_total)
    )
    allowed = (key_pos[None, :] <= query_pos[:, None]) | (key_frames[None, :] == query_frames[:, None])

    scores = (
        jnp.einsum("qhd,kd->hqk", query_heads, key_all, preferred_element_type=jnp.float32)
        * scale_factor
    )
    masked_scores = jnp.where(allowed[None], scores, MASKED)
    running = masked_scores.max(axis=-1)
    summed = jnp.exp(masked_scores - running[:, :, None]).sum(axis=-1)
    log_total = running + jnp.log(summed)

    probability = jnp.exp(jnp.where(allowed[None], scores - log_total[:, :, None], MASKED))
    probs_low = probability.astype(jnp.bfloat16)
    grad_probs = jnp.einsum(
        "qhd,kd->hqk", grad_heads, value_all, preferred_element_type=jnp.float32
    )
    grad_scores = (probability * (grad_probs - corrections[:, :, None])).astype(jnp.bfloat16)
    grad_query = (
        jnp.einsum("hqk,kd->qhd", grad_scores, key_all, preferred_element_type=jnp.float32)
        * scale_factor
    )
    key_part = (
        jnp.einsum("hqk,qhd->kd", grad_scores, query_heads, preferred_element_type=jnp.float32)
        * scale_factor
    )
    value_part = jnp.einsum(
        "hqk,qhd->kd", probs_low, grad_heads, preferred_element_type=jnp.float32
    )
    summed_grads = lax.psum_scatter(
        lax.psum_scatter(
            jnp.concatenate([key_part, value_part], axis=1).astype(jnp.bfloat16),
            "cy",
            scatter_dimension=0,
            tiled=True,
        ).astype(jnp.float32),
        "cz",
        scatter_dimension=0,
        tiled=True,
    )
    grad_keys_low = summed_grads[:, :HEAD_DIM].astype(jnp.bfloat16)
    grad_values_low = summed_grads[:, HEAD_DIM:].astype(jnp.bfloat16)
    grad_query_low = grad_query.astype(jnp.bfloat16).reshape(local_rows, GROUP * HEAD_DIM)
    visual_picks = visual_rows[0, 0]
    chosen = jnp.concatenate(
        [grad_query_low[visual_picks], grad_keys_low[visual_picks], grad_values_low[visual_picks]],
        axis=1,
    )
    everyone = lax.all_gather(chosen[None], ("section", "dp"), axis=0, tiled=True)
    groups = lax.axis_size("section")
    replicas = lax.axis_size("dp")
    half_rows = visual_picks.shape[0] // 2
    width_in = chosen.shape[1]
    arranged = (
        everyone.reshape(groups, replicas, 2, half_rows, width_in)
        .transpose(2, 1, 3, 0, 4)
        .reshape(2 * replicas * half_rows, groups * width_in)
    )
    visual_grad = jnp.dot(arranged, qkv_weight, preferred_element_type=jnp.float32).astype(
        jnp.bfloat16
    )
    shuffled = lax.psum_scatter(
        jnp.dot(visual_grad, projector_weight, preferred_element_type=jnp.float32).astype(
            jnp.bfloat16
        ),
        ("section", "dp"),
        scatter_dimension=0,
        tiled=True,
    ).astype(jnp.float32)
    slot_rows = shuffled.reshape(half_rows * 4, projector_weight.shape[1] // 4)
    patches = slot_rows[shuffle_source[0, 0]].astype(jnp.bfloat16)
    return (grad_keys_low[None], grad_values_low[None], patches[None])


def solution(mesh):
    ctx_size = mesh.shape["ctx"]
    ring_y = 8 if ctx_size % 8 == 0 else 1
    split_mesh = jax.sharding.Mesh(
        mesh.devices.reshape(
            ctx_size // ring_y, ring_y, mesh.shape["section"], mesh.shape["dp"]
        ),
        ("cz", "cy", "section", "dp"),
    )
    ctx = ("cz", "cy")
    placed = (
        P("dp", ctx, "section"),
        P("dp", ctx, "section"),
        P("dp", ctx, "section"),
        P("dp", ctx, "section"),
        P("dp", "section", ctx),
        P("dp", None),
        P("dp", ctx, None),
        P("dp", ("cz", "cy", "section"), None),
        P(None, ("section", "dp")),
        P(("section", "dp"), None),
    )
    return jax.shard_map(
        shards,
        mesh=split_mesh,
        in_specs=placed,
        out_specs=(
            P("dp", ctx, "section"),
            P("dp", ctx, "section"),
            P("dp", ("cz", "cy", "section"), None),
        ),
        check_vma=False,
    )
```

```python
import math

import jax
import jax.numpy as jnp
from jax import lax
from jax.sharding import PartitionSpec as P

HEAD_DIM = 128
GROUP = 7


MASKED = -1e30


def shards(
    query_vectors,
    key_vectors,
    value_vectors,
    grad_output,
    output_dots,
    frame_ids,
    visual_rows,
    shuffle_source,
    qkv_weight,
    projector_weight,
):
    ring_z = lax.axis_size("cz")
    ring_y = lax.axis_size("cy")
    position = lax.axis_index("cz") * ring_y + lax.axis_index("cy")
    local_rows = query_vectors.shape[1]
    scale_factor = 1.0 / math.sqrt(HEAD_DIM)
    query_heads = query_vectors[0].reshape(local_rows, GROUP, HEAD_DIM)
    grad_heads = grad_output[0].reshape(local_rows, GROUP, HEAD_DIM)
    corrections = output_dots[0]
    frame_line = frame_ids[0]
    seq_total = frame_line.shape[0]
    query_first = position * local_rows
    query_pos = query_first + jnp.arange(local_rows, dtype=jnp.int32)
    query_frames = lax.dynamic_slice_in_dim(frame_line, query_first, local_rows)

    own_pair = jnp.concatenate([key_vectors[0], value_vectors[0]], axis=1)
    all_pairs = lax.all_gather(
        lax.all_gather(own_pair, "cz", axis=0, tiled=True), "cy", axis=0, tiled=True
    )
    key_all = all_pairs[:, :HEAD_DIM]
    value_all = all_pairs[:, HEAD_DIM:]

    key_pos = (
        jnp.arange(seq_total, dtype=jnp.int32)
        .reshape(ring_z, ring_y, local_rows)
        .transpose(1, 0, 2)
        .reshape(seq_total)
    )
    key_frames = (
        frame_line.reshape(ring_z, ring_y, local_rows).transpose(1, 0, 2).reshape(seq_total)
    )
    allowed = (key_pos[None, :] <= query_pos[:, None]) | (key_frames[None, :] == query_frames[:, None])

    scores = (
        jnp.einsum("qhd,kd->hqk", query_heads, key_all, preferred_element_type=jnp.float32)
        * scale_factor
    )
    masked_scores = jnp.where(allowed[None], scores, MASKED)
    running = masked_scores.max(axis=-1)
    summed = jnp.exp(masked_scores - running[:, :, None]).sum(axis=-1)
    log_total = running + jnp.log(summed)

    probability = jnp.exp(jnp.where(allowed[None], scores - log_total[:, :, None], MASKED))
    probs_low = probability.astype(jnp.bfloat16)
    grad_probs = jnp.einsum(
        "qhd,kd->hqk", grad_heads, value_all, preferred_element_type=jnp.float32
    )
    grad_scores = (probability * (grad_probs - corrections[:, :, None])).astype(jnp.bfloat16)
    grad_query = (
        jnp.einsum("hqk,kd->qhd", grad_scores, key_all, preferred_element_type=jnp.float32)
        * scale_factor
    )
    key_part = (
        jnp.einsum("hqk,qhd->kd", grad_scores, query_heads, preferred_element_type=jnp.float32)
        * scale_factor
    )
    value_part = jnp.einsum(
        "hqk,qhd->kd", probs_low, grad_heads, preferred_element_type=jnp.float32
    )
    summed_grads = lax.psum_scatter(
        lax.psum_scatter(
            jnp.concatenate([key_part, value_part], axis=1).astype(jnp.bfloat16),
            "cy",
            scatter_dimension=0,
            tiled=True,
        ).astype(jnp.float32),
        "cz",
        scatter_dimension=0,
        tiled=True,
    )
    grad_keys_low = summed_grads[:, :HEAD_DIM].astype(jnp.bfloat16)
    grad_values_low = summed_grads[:, HEAD_DIM:].astype(jnp.bfloat16)
    grad_query_low = grad_query.astype(jnp.bfloat16).reshape(local_rows, GROUP * HEAD_DIM)
    visual_picks = visual_rows[0, 0]
    chosen = jnp.concatenate(
        [grad_query_low[visual_picks], grad_keys_low[visual_picks], grad_values_low[visual_picks]],
        axis=1,
    )
    everyone = lax.all_gather(chosen[None], ("section", "dp"), axis=0, tiled=True)
    groups = lax.axis_size("section")
    replicas = lax.axis_size("dp")
    half_rows = visual_picks.shape[0] // 2
    width_in = chosen.shape[1]
    arranged = (
        everyone.reshape(groups, replicas, 2, half_rows, width_in)
        .transpose(2, 1, 3, 0, 4)
        .reshape(2 * replicas * half_rows, groups * width_in)
    )
    visual_grad = jnp.dot(arranged, qkv_weight, preferred_element_type=jnp.float32).astype(
        jnp.bfloat16
    )
    pieces = lax.all_to_all(
        jnp.dot(visual_grad, projector_weight, preferred_element_type=jnp.float32).astype(
            jnp.bfloat16
        ),
        ("section", "dp"),
        0,
        0,
        tiled=True,
    )
    shuffled = pieces.astype(jnp.float32).reshape(groups * replicas, -1, pieces.shape[1]).sum(0)
    slot_rows = shuffled.reshape(half_rows * 4, projector_weight.shape[1] // 4)
    patches = slot_rows[shuffle_source[0, 0]].astype(jnp.bfloat16)
    return (grad_keys_low[None], grad_values_low[None], patches[None])


def solution(mesh):
    ctx_size = mesh.shape["ctx"]
    ring_y = 8 if ctx_size % 8 == 0 else 1
    split_mesh = jax.sharding.Mesh(
        mesh.devices.reshape(
            ctx_size // ring_y, ring_y, mesh.shape["section"], mesh.shape["dp"]
        ),
        ("cz", "cy", "section", "dp"),
    )
    ctx = ("cz", "cy")
    placed = (
        P("dp", ctx, "section"),
        P("dp", ctx, "section"),
        P("dp", ctx, "section"),
        P("dp", ctx, "section"),
        P("dp", "section", ctx),
        P("dp", None),
        P("dp", ctx, None),
        P("dp", ("cz", "cy", "section"), None),
        P(None, ("section", "dp")),
        P(("section", "dp"), None),
    )
    return jax.shard_map(
        shards,
        mesh=split_mesh,
        in_specs=placed,
        out_specs=(
            P("dp", ctx, "section"),
            P("dp", ctx, "section"),
            P("dp", ("cz", "cy", "section"), None),
        ),
        check_vma=False,
    )
```

```python
import math

import jax
import jax.numpy as jnp
from jax import lax
from jax.sharding import PartitionSpec as P

HEAD_DIM = 128
GROUP = 7


MASKED = -1e30


def shards(
    query_vectors,
    key_vectors,
    value_vectors,
    grad_output,
    output_dots,
    frame_ids,
    visual_rows,
    shuffle_source,
    qkv_weight,
    projector_weight,
):
    ring_z = lax.axis_size("cz")
    ring_y = lax.axis_size("cy")
    position = lax.axis_index("cz") * ring_y + lax.axis_index("cy")
    local_rows = query_vectors.shape[1]
    scale_factor = 1.0 / math.sqrt(HEAD_DIM)
    query_heads = query_vectors[0].reshape(local_rows, GROUP, HEAD_DIM)
    grad_heads = grad_output[0].reshape(local_rows, GROUP, HEAD_DIM)
    corrections = output_dots[0]
    frame_line = frame_ids[0]
    seq_total = frame_line.shape[0]
    query_first = position * local_rows
    query_pos = query_first + jnp.arange(local_rows, dtype=jnp.int32)
    query_frames = lax.dynamic_slice_in_dim(frame_line, query_first, local_rows)

    own_pair = jnp.concatenate([key_vectors[0], value_vectors[0]], axis=1)
    all_pairs = lax.all_gather(
        lax.all_to_all(jnp.tile(own_pair, (ring_z, 1)), "cz", 0, 0, tiled=True),
        "cy",
        axis=0,
        tiled=True,
    )
    key_all = all_pairs[:, :HEAD_DIM]
    value_all = all_pairs[:, HEAD_DIM:]

    key_pos = (
        jnp.arange(seq_total, dtype=jnp.int32)
        .reshape(ring_z, ring_y, local_rows)
        .transpose(1, 0, 2)
        .reshape(seq_total)
    )
    key_frames = (
        frame_line.reshape(ring_z, ring_y, local_rows).transpose(1, 0, 2).reshape(seq_total)
    )
    allowed = (key_pos[None, :] <= query_pos[:, None]) | (key_frames[None, :] == query_frames[:, None])

    scores = (
        jnp.einsum("qhd,kd->hqk", query_heads, key_all, preferred_element_type=jnp.float32)
        * scale_factor
    )
    masked_scores = jnp.where(allowed[None], scores, MASKED)
    running = masked_scores.max(axis=-1)
    summed = jnp.exp(masked_scores - running[:, :, None]).sum(axis=-1)
    log_total = running + jnp.log(summed)

    probability = jnp.exp(jnp.where(allowed[None], scores - log_total[:, :, None], MASKED))
    probs_low = probability.astype(jnp.bfloat16)
    grad_probs = jnp.einsum(
        "qhd,kd->hqk", grad_heads, value_all, preferred_element_type=jnp.float32
    )
    grad_scores = (probability * (grad_probs - corrections[:, :, None])).astype(jnp.bfloat16)
    grad_query = (
        jnp.einsum("hqk,kd->qhd", grad_scores, key_all, preferred_element_type=jnp.float32)
        * scale_factor
    )
    key_part = (
        jnp.einsum("hqk,qhd->kd", grad_scores, query_heads, preferred_element_type=jnp.float32)
        * scale_factor
    )
    value_part = jnp.einsum(
        "hqk,qhd->kd", probs_low, grad_heads, preferred_element_type=jnp.float32
    )
    stage_one = lax.psum_scatter(
        jnp.concatenate([key_part, value_part], axis=1).astype(jnp.bfloat16),
        "cy",
        scatter_dimension=0,
        tiled=True,
    )
    stage_two = lax.all_to_all(stage_one, "cz", 0, 0, tiled=True)
    summed_grads = (
        stage_two.astype(jnp.float32).reshape(ring_z, local_rows, stage_two.shape[1]).sum(0)
    )
    grad_keys_low = summed_grads[:, :HEAD_DIM].astype(jnp.bfloat16)
    grad_values_low = summed_grads[:, HEAD_DIM:].astype(jnp.bfloat16)
    grad_query_low = grad_query.astype(jnp.bfloat16).reshape(local_rows, GROUP * HEAD_DIM)
    visual_picks = visual_rows[0, 0]
    chosen = jnp.concatenate(
        [grad_query_low[visual_picks], grad_keys_low[visual_picks], grad_values_low[visual_picks]],
        axis=1,
    )
    everyone = lax.all_gather(chosen[None], ("section", "dp"), axis=0, tiled=True)
    groups = lax.axis_size("section")
    replicas = lax.axis_size("dp")
    half_rows = visual_picks.shape[0] // 2
    width_in = chosen.shape[1]
    arranged = (
        everyone.reshape(groups, replicas, 2, half_rows, width_in)
        .transpose(2, 1, 3, 0, 4)
        .reshape(2 * replicas * half_rows, groups * width_in)
    )
    visual_grad = jnp.dot(arranged, qkv_weight, preferred_element_type=jnp.float32).astype(
        jnp.bfloat16
    )
    pieces = lax.all_to_all(
        jnp.dot(visual_grad, projector_weight, preferred_element_type=jnp.float32).astype(
            jnp.bfloat16
        ),
        ("section", "dp"),
        0,
        0,
        tiled=True,
    )
    shuffled = pieces.astype(jnp.float32).reshape(groups * replicas, -1, pieces.shape[1]).sum(0)
    slot_rows = shuffled.reshape(half_rows * 4, projector_weight.shape[1] // 4)
    patches = slot_rows[shuffle_source[0, 0]].astype(jnp.bfloat16)
    return (grad_keys_low[None], grad_values_low[None], patches[None])


def solution(mesh):
    ctx_size = mesh.shape["ctx"]
    ring_y = 8 if ctx_size % 8 == 0 else 1
    split_mesh = jax.sharding.Mesh(
        mesh.devices.reshape(
            ctx_size // ring_y, ring_y, mesh.shape["section"], mesh.shape["dp"]
        ),
        ("cz", "cy", "section", "dp"),
    )
    ctx = ("cz", "cy")
    placed = (
        P("dp", ctx, "section"),
        P("dp", ctx, "section"),
        P("dp", ctx, "section"),
        P("dp", ctx, "section"),
        P("dp", "section", ctx),
        P("dp", None),
        P("dp", ctx, None),
        P("dp", ("cz", "cy", "section"), None),
        P(None, ("section", "dp")),
        P(("section", "dp"), None),
    )
    return jax.shard_map(
        shards,
        mesh=split_mesh,
        in_specs=placed,
        out_specs=(
            P("dp", ctx, "section"),
            P("dp", ctx, "section"),
            P("dp", ("cz", "cy", "section"), None),
        ),
        check_vma=False,
    )
```

```python
import math

import jax
import jax.numpy as jnp
from jax import lax
from jax.experimental import pallas as pl
from jax.experimental.pallas import tpu as pltpu
from jax.sharding import PartitionSpec as P

HEAD_DIM = 128
GROUP = 7


MASKED = -1e30
KEY_TILE = 512
INTERPRET = False


def backward_kernel(
    q_ref, g_ref, dots_ref, qpos_ref, qframe_ref, kv_ref, kpos_ref, kframe_ref, dq_ref, dkv_ref
):
    rows = q_ref.shape[0]
    tiles = kpos_ref.shape[0]
    scale_factor = 1.0 / math.sqrt(HEAD_DIM)
    query_block = q_ref[...]
    grad_block = g_ref[...]
    qpos = qpos_ref[...]
    qframe = qframe_ref[...]

    def allowed_at(tile):
        kpos = kpos_ref[pl.ds(tile, 1), :]
        kframe = kframe_ref[pl.ds(tile, 1), :]
        return (kpos <= qpos) | (kframe == qframe)

    def scores_at(tile):
        start = pl.multiple_of(tile * KEY_TILE, KEY_TILE)
        keys = kv_ref[pl.ds(start, KEY_TILE), pl.ds(0, HEAD_DIM)]
        return (
            lax.dot_general(
                query_block, keys, (((1,), (1,)), ((), ())), preferred_element_type=jnp.float32
            )
            * scale_factor
        )

    def statistics(tile, carried):
        running, summed = carried
        scores = jnp.where(allowed_at(tile), scores_at(tile), MASKED)
        newest = jnp.maximum(running, scores.max(axis=1, keepdims=True))
        summed = summed * jnp.exp(running - newest) + jnp.exp(scores - newest).sum(
            axis=1, keepdims=True
        )
        return (newest, summed)

    running, summed = lax.fori_loop(
        0,
        tiles,
        statistics,
        (jnp.full((rows, 1), MASKED, jnp.float32), jnp.zeros((rows, 1), jnp.float32)),
    )
    log_total = running + jnp.log(summed)
    dots = dots_ref[...]

    def gradients(tile, query_now):
        start = pl.multiple_of(tile * KEY_TILE, KEY_TILE)
        keys = kv_ref[pl.ds(start, KEY_TILE), pl.ds(0, HEAD_DIM)]
        values = kv_ref[pl.ds(start, KEY_TILE), pl.ds(HEAD_DIM, HEAD_DIM)]
        probability = jnp.exp(jnp.where(allowed_at(tile), scores_at(tile) - log_total, MASKED))
        grad_probs = lax.dot_general(
            grad_block, values, (((1,), (1,)), ((), ())), preferred_element_type=jnp.float32
        )
        grad_scores = (probability * (grad_probs - dots)).astype(jnp.bfloat16)
        key_part = (
            jnp.dot(grad_scores.T, query_block, preferred_element_type=jnp.float32) * scale_factor
        )
        value_part = jnp.dot(
            probability.astype(jnp.bfloat16).T, grad_block, preferred_element_type=jnp.float32
        )
        dkv_ref[pl.ds(start, KEY_TILE), pl.ds(0, HEAD_DIM)] = key_part.astype(dkv_ref.dtype)
        dkv_ref[pl.ds(start, KEY_TILE), pl.ds(HEAD_DIM, HEAD_DIM)] = value_part.astype(
            dkv_ref.dtype
        )
        return query_now + jnp.dot(grad_scores, keys, preferred_element_type=jnp.float32)

    query_now = lax.fori_loop(0, tiles, gradients, jnp.zeros((rows, HEAD_DIM), jnp.float32))
    dq_ref[...] = query_now * scale_factor


def attention_backward(q2, g2, dots2, qpos2, qframe2, kv, kpos2, kframe2):
    rows = q2.shape[0]
    return pl.pallas_call(
        backward_kernel,
        out_shape=(
            jax.ShapeDtypeStruct((rows, HEAD_DIM), jnp.float32),
            jax.ShapeDtypeStruct(kv.shape, jnp.bfloat16),
        ),
        interpret=INTERPRET,
    )(q2, g2, dots2, qpos2, qframe2, kv, kpos2, kframe2)


def shards(
    query_vectors,
    key_vectors,
    value_vectors,
    grad_output,
    output_dots,
    frame_ids,
    visual_rows,
    shuffle_source,
    qkv_weight,
    projector_weight,
):
    ring_z = lax.axis_size("cz")
    ring_y = lax.axis_size("cy")
    position = lax.axis_index("cz") * ring_y + lax.axis_index("cy")
    local_rows = query_vectors.shape[1]
    scale_factor = 1.0 / math.sqrt(HEAD_DIM)
    query_heads = query_vectors[0].reshape(local_rows, GROUP, HEAD_DIM)
    grad_heads = grad_output[0].reshape(local_rows, GROUP, HEAD_DIM)
    corrections = output_dots[0]
    frame_line = frame_ids[0]
    seq_total = frame_line.shape[0]
    query_first = position * local_rows
    query_pos = query_first + jnp.arange(local_rows, dtype=jnp.int32)
    query_frames = lax.dynamic_slice_in_dim(frame_line, query_first, local_rows)

    own_pair = jnp.concatenate([key_vectors[0], value_vectors[0]], axis=1)
    all_pairs = lax.all_gather(
        lax.all_to_all(jnp.tile(own_pair, (ring_z, 1)), "cz", 0, 0, tiled=True),
        "cy",
        axis=0,
        tiled=True,
    )

    key_pos = (
        jnp.arange(seq_total, dtype=jnp.int32)
        .reshape(ring_z, ring_y, local_rows)
        .transpose(1, 0, 2)
        .reshape(seq_total)
    )
    key_frames = (
        frame_line.reshape(ring_z, ring_y, local_rows).transpose(1, 0, 2).reshape(seq_total)
    )
    rows = GROUP * local_rows
    q2 = query_heads.transpose(1, 0, 2).reshape(rows, HEAD_DIM)
    g2 = grad_heads.transpose(1, 0, 2).reshape(rows, HEAD_DIM)
    dots2 = corrections.reshape(rows, 1)
    qpos2 = jnp.tile(query_pos, GROUP).reshape(rows, 1)
    qframe2 = jnp.tile(query_frames, GROUP).reshape(rows, 1)
    tiles = seq_total // KEY_TILE
    dq2, partials = attention_backward(
        q2,
        g2,
        dots2,
        qpos2,
        qframe2,
        all_pairs,
        key_pos.reshape(tiles, KEY_TILE),
        key_frames.reshape(tiles, KEY_TILE),
    )
    grad_query = dq2.reshape(GROUP, local_rows, HEAD_DIM).transpose(1, 0, 2)
    stage_one = lax.psum_scatter(
        partials,
        "cy",
        scatter_dimension=0,
        tiled=True,
    )
    stage_two = lax.all_to_all(stage_one, "cz", 0, 0, tiled=True)
    summed_grads = (
        stage_two.astype(jnp.float32).reshape(ring_z, local_rows, stage_two.shape[1]).sum(0)
    )
    grad_keys_low = summed_grads[:, :HEAD_DIM].astype(jnp.bfloat16)
    grad_values_low = summed_grads[:, HEAD_DIM:].astype(jnp.bfloat16)
    grad_query_low = grad_query.astype(jnp.bfloat16).reshape(local_rows, GROUP * HEAD_DIM)
    visual_picks = visual_rows[0, 0]
    chosen = jnp.concatenate(
        [grad_query_low[visual_picks], grad_keys_low[visual_picks], grad_values_low[visual_picks]],
        axis=1,
    )
    everyone = lax.all_gather(chosen[None], ("section", "dp"), axis=0, tiled=True)
    groups = lax.axis_size("section")
    replicas = lax.axis_size("dp")
    half_rows = visual_picks.shape[0] // 2
    width_in = chosen.shape[1]
    arranged = (
        everyone.reshape(groups, replicas, 2, half_rows, width_in)
        .transpose(2, 1, 3, 0, 4)
        .reshape(2 * replicas * half_rows, groups * width_in)
    )
    visual_grad = jnp.dot(arranged, qkv_weight, preferred_element_type=jnp.float32).astype(
        jnp.bfloat16
    )
    pieces = lax.all_to_all(
        jnp.dot(visual_grad, projector_weight, preferred_element_type=jnp.float32).astype(
            jnp.bfloat16
        ),
        ("section", "dp"),
        0,
        0,
        tiled=True,
    )
    shuffled = pieces.astype(jnp.float32).reshape(groups * replicas, -1, pieces.shape[1]).sum(0)
    slot_rows = shuffled.reshape(half_rows * 4, projector_weight.shape[1] // 4)
    patches = slot_rows[shuffle_source[0, 0]].astype(jnp.bfloat16)
    return (grad_keys_low[None], grad_values_low[None], patches[None])


def solution(mesh):
    ctx_size = mesh.shape["ctx"]
    ring_y = 8 if ctx_size % 8 == 0 else 1
    split_mesh = jax.sharding.Mesh(
        mesh.devices.reshape(
            ctx_size // ring_y, ring_y, mesh.shape["section"], mesh.shape["dp"]
        ),
        ("cz", "cy", "section", "dp"),
    )
    ctx = ("cz", "cy")
    placed = (
        P("dp", ctx, "section"),
        P("dp", ctx, "section"),
        P("dp", ctx, "section"),
        P("dp", ctx, "section"),
        P("dp", "section", ctx),
        P("dp", None),
        P("dp", ctx, None),
        P("dp", ("cz", "cy", "section"), None),
        P(None, ("section", "dp")),
        P(("section", "dp"), None),
    )
    return jax.shard_map(
        shards,
        mesh=split_mesh,
        in_specs=placed,
        out_specs=(
            P("dp", ctx, "section"),
            P("dp", ctx, "section"),
            P("dp", ("cz", "cy", "section"), None),
        ),
        check_vma=False,
    )
```

```python
import math

import jax
import jax.numpy as jnp
from jax import lax
from jax.experimental import pallas as pl
from jax.experimental.pallas import tpu as pltpu
from jax.sharding import PartitionSpec as P

HEAD_DIM = 128
GROUP = 7


MASKED = -1e30
KEY_TILE = 512
INTERPRET = False


def backward_kernel(
    q_ref, g_ref, dots_ref, qpos_ref, qframe_ref, kv_ref, kpos_ref, kframe_ref, dq_ref, dkv_ref
):
    rows = q_ref.shape[0]
    local_rows = qpos_ref.shape[0]
    heads = rows // local_rows
    tiles = kpos_ref.shape[0]
    scale_factor = 1.0 / math.sqrt(HEAD_DIM)
    query_block = q_ref[...]
    grad_block = g_ref[...]
    qpos = qpos_ref[...]
    qframe = qframe_ref[...]

    def allowed_at(tile):
        kpos = kpos_ref[pl.ds(tile, 1), :]
        kframe = kframe_ref[pl.ds(tile, 1), :]
        return ((kpos <= qpos) | (kframe == qframe))[None]

    def scores_at(tile):
        start = pl.multiple_of(tile * KEY_TILE, KEY_TILE)
        keys = kv_ref[pl.ds(start, KEY_TILE), pl.ds(0, HEAD_DIM)]
        scores = (
            lax.dot_general(
                query_block, keys, (((1,), (1,)), ((), ())), preferred_element_type=jnp.float32
            )
            * scale_factor
        )
        return scores.reshape(heads, local_rows, KEY_TILE)

    def statistics(tile, carried):
        running, summed = carried
        scores = jnp.where(allowed_at(tile), scores_at(tile), MASKED)
        newest = jnp.maximum(running, scores.max(axis=2, keepdims=True))
        summed = summed * jnp.exp(running - newest) + jnp.exp(scores - newest).sum(
            axis=2, keepdims=True
        )
        return (newest, summed)

    running, summed = lax.fori_loop(
        0,
        tiles,
        statistics,
        (
            jnp.full((heads, local_rows, 1), MASKED, jnp.float32),
            jnp.zeros((heads, local_rows, 1), jnp.float32),
        ),
    )
    log_total = running + jnp.log(summed)
    dots = dots_ref[...].reshape(heads, local_rows, 1)

    def gradients(tile, query_now):
        start = pl.multiple_of(tile * KEY_TILE, KEY_TILE)
        keys = kv_ref[pl.ds(start, KEY_TILE), pl.ds(0, HEAD_DIM)]
        values = kv_ref[pl.ds(start, KEY_TILE), pl.ds(HEAD_DIM, HEAD_DIM)]
        probability = jnp.exp(jnp.where(allowed_at(tile), scores_at(tile) - log_total, MASKED))
        grad_probs = lax.dot_general(
            grad_block, values, (((1,), (1,)), ((), ())), preferred_element_type=jnp.float32
        ).reshape(heads, local_rows, KEY_TILE)
        grad_scores = (
            (probability * (grad_probs - dots)).astype(jnp.bfloat16).reshape(rows, KEY_TILE)
        )
        probs_low = probability.astype(jnp.bfloat16).reshape(rows, KEY_TILE)
        key_part = (
            jnp.dot(grad_scores.T, query_block, preferred_element_type=jnp.float32) * scale_factor
        )
        value_part = jnp.dot(probs_low.T, grad_block, preferred_element_type=jnp.float32)
        dkv_ref[pl.ds(start, KEY_TILE), pl.ds(0, HEAD_DIM)] = key_part.astype(dkv_ref.dtype)
        dkv_ref[pl.ds(start, KEY_TILE), pl.ds(HEAD_DIM, HEAD_DIM)] = value_part.astype(
            dkv_ref.dtype
        )
        return query_now + jnp.dot(grad_scores, keys, preferred_element_type=jnp.float32)

    query_now = lax.fori_loop(0, tiles, gradients, jnp.zeros((rows, HEAD_DIM), jnp.float32))
    dq_ref[...] = query_now * scale_factor


def attention_backward(q2, g2, dots2, qpos2, qframe2, kv, kpos2, kframe2):
    rows = q2.shape[0]
    return pl.pallas_call(
        backward_kernel,
        out_shape=(
            jax.ShapeDtypeStruct((rows, HEAD_DIM), jnp.float32),
            jax.ShapeDtypeStruct(kv.shape, jnp.bfloat16),
        ),
        interpret=INTERPRET,
    )(q2, g2, dots2, qpos2, qframe2, kv, kpos2, kframe2)


def shards(
    query_vectors,
    key_vectors,
    value_vectors,
    grad_output,
    output_dots,
    frame_ids,
    visual_rows,
    shuffle_source,
    qkv_weight,
    projector_weight,
):
    ring_z = lax.axis_size("cz")
    ring_y = lax.axis_size("cy")
    position = lax.axis_index("cz") * ring_y + lax.axis_index("cy")
    local_rows = query_vectors.shape[1]
    scale_factor = 1.0 / math.sqrt(HEAD_DIM)
    query_heads = query_vectors[0].reshape(local_rows, GROUP, HEAD_DIM)
    grad_heads = grad_output[0].reshape(local_rows, GROUP, HEAD_DIM)
    corrections = output_dots[0]
    frame_line = frame_ids[0]
    seq_total = frame_line.shape[0]
    query_first = position * local_rows
    query_pos = query_first + jnp.arange(local_rows, dtype=jnp.int32)
    query_frames = lax.dynamic_slice_in_dim(frame_line, query_first, local_rows)

    own_pair = jnp.concatenate([key_vectors[0], value_vectors[0]], axis=1)
    all_pairs = lax.all_gather(
        lax.all_to_all(jnp.tile(own_pair, (ring_z, 1)), "cz", 0, 0, tiled=True),
        "cy",
        axis=0,
        tiled=True,
    )

    key_pos = (
        jnp.arange(seq_total, dtype=jnp.int32)
        .reshape(ring_z, ring_y, local_rows)
        .transpose(1, 0, 2)
        .reshape(seq_total)
    )
    key_frames = (
        frame_line.reshape(ring_z, ring_y, local_rows).transpose(1, 0, 2).reshape(seq_total)
    )
    rows = GROUP * local_rows
    q2 = query_heads.transpose(1, 0, 2).reshape(rows, HEAD_DIM)
    g2 = grad_heads.transpose(1, 0, 2).reshape(rows, HEAD_DIM)
    dots2 = corrections.reshape(rows, 1)
    qpos2 = query_pos.reshape(local_rows, 1)
    qframe2 = query_frames.reshape(local_rows, 1)
    tiles = seq_total // KEY_TILE
    dq2, partials = attention_backward(
        q2,
        g2,
        dots2,
        qpos2,
        qframe2,
        all_pairs,
        key_pos.reshape(tiles, KEY_TILE),
        key_frames.reshape(tiles, KEY_TILE),
    )
    grad_query = dq2.reshape(GROUP, local_rows, HEAD_DIM).transpose(1, 0, 2)
    stage_one = lax.psum_scatter(
        partials,
        "cy",
        scatter_dimension=0,
        tiled=True,
    )
    stage_two = lax.all_to_all(stage_one, "cz", 0, 0, tiled=True)
    summed_grads = (
        stage_two.astype(jnp.float32).reshape(ring_z, local_rows, stage_two.shape[1]).sum(0)
    )
    grad_keys_low = summed_grads[:, :HEAD_DIM].astype(jnp.bfloat16)
    grad_values_low = summed_grads[:, HEAD_DIM:].astype(jnp.bfloat16)
    grad_query_low = grad_query.astype(jnp.bfloat16).reshape(local_rows, GROUP * HEAD_DIM)
    visual_picks = visual_rows[0, 0]
    chosen = jnp.concatenate(
        [grad_query_low[visual_picks], grad_keys_low[visual_picks], grad_values_low[visual_picks]],
        axis=1,
    )
    everyone = lax.all_gather(chosen[None], ("section", "dp"), axis=0, tiled=True)
    groups = lax.axis_size("section")
    replicas = lax.axis_size("dp")
    half_rows = visual_picks.shape[0] // 2
    width_in = chosen.shape[1]
    arranged = (
        everyone.reshape(groups, replicas, 2, half_rows, width_in)
        .transpose(2, 1, 3, 0, 4)
        .reshape(2 * replicas * half_rows, groups * width_in)
    )
    visual_grad = jnp.dot(arranged, qkv_weight, preferred_element_type=jnp.float32).astype(
        jnp.bfloat16
    )
    pieces = lax.all_to_all(
        jnp.dot(visual_grad, projector_weight, preferred_element_type=jnp.float32).astype(
            jnp.bfloat16
        ),
        ("section", "dp"),
        0,
        0,
        tiled=True,
    )
    shuffled = pieces.astype(jnp.float32).reshape(groups * replicas, -1, pieces.shape[1]).sum(0)
    slot_rows = shuffled.reshape(half_rows * 4, projector_weight.shape[1] // 4)
    patches = slot_rows[shuffle_source[0, 0]].astype(jnp.bfloat16)
    return (grad_keys_low[None], grad_values_low[None], patches[None])


def solution(mesh):
    ctx_size = mesh.shape["ctx"]
    ring_y = 8 if ctx_size % 8 == 0 else 1
    split_mesh = jax.sharding.Mesh(
        mesh.devices.reshape(
            ctx_size // ring_y, ring_y, mesh.shape["section"], mesh.shape["dp"]
        ),
        ("cz", "cy", "section", "dp"),
    )
    ctx = ("cz", "cy")
    placed = (
        P("dp", ctx, "section"),
        P("dp", ctx, "section"),
        P("dp", ctx, "section"),
        P("dp", ctx, "section"),
        P("dp", "section", ctx),
        P("dp", None),
        P("dp", ctx, None),
        P("dp", ("cz", "cy", "section"), None),
        P(None, ("section", "dp")),
        P(("section", "dp"), None),
    )
    return jax.shard_map(
        shards,
        mesh=split_mesh,
        in_specs=placed,
        out_specs=(
            P("dp", ctx, "section"),
            P("dp", ctx, "section"),
            P("dp", ("cz", "cy", "section"), None),
        ),
        check_vma=False,
    )
```

```python
import math

import jax
import jax.numpy as jnp
from jax import lax
from jax.experimental import pallas as pl
from jax.experimental.pallas import tpu as pltpu
from jax.sharding import PartitionSpec as P

HEAD_DIM = 128
GROUP = 7


MASKED = -1e30
KEY_TILE = 2048
INTERPRET = False


def backward_kernel(
    q_ref, g_ref, dots_ref, qpos_ref, qframe_ref, kv_ref, kpos_ref, kframe_ref, dq_ref, dkv_ref
):
    rows = q_ref.shape[0]
    local_rows = qpos_ref.shape[0]
    heads = rows // local_rows
    tiles = kpos_ref.shape[0]
    scale_factor = 1.0 / math.sqrt(HEAD_DIM)
    query_block = q_ref[...]
    grad_block = g_ref[...]
    qpos = qpos_ref[...]
    qframe = qframe_ref[...]

    def allowed_at(tile):
        kpos = kpos_ref[pl.ds(tile, 1), :]
        kframe = kframe_ref[pl.ds(tile, 1), :]
        return ((kpos <= qpos) | (kframe == qframe))[None]

    def scores_at(tile):
        start = pl.multiple_of(tile * KEY_TILE, KEY_TILE)
        keys = kv_ref[pl.ds(start, KEY_TILE), pl.ds(0, HEAD_DIM)]
        scores = (
            lax.dot_general(
                query_block, keys, (((1,), (1,)), ((), ())), preferred_element_type=jnp.float32
            )
            * scale_factor
        )
        return scores.reshape(heads, local_rows, KEY_TILE)

    def statistics(tile, carried):
        running, summed = carried
        scores = jnp.where(allowed_at(tile), scores_at(tile), MASKED)
        newest = jnp.maximum(running, scores.max(axis=2, keepdims=True))
        summed = summed * jnp.exp(running - newest) + jnp.exp(scores - newest).sum(
            axis=2, keepdims=True
        )
        return (newest, summed)

    running, summed = lax.fori_loop(
        0,
        tiles,
        statistics,
        (
            jnp.full((heads, local_rows, 1), MASKED, jnp.float32),
            jnp.zeros((heads, local_rows, 1), jnp.float32),
        ),
    )
    log_total = running + jnp.log(summed)
    dots = dots_ref[...].reshape(heads, local_rows, 1)

    def gradients(tile, query_now):
        start = pl.multiple_of(tile * KEY_TILE, KEY_TILE)
        keys = kv_ref[pl.ds(start, KEY_TILE), pl.ds(0, HEAD_DIM)]
        values = kv_ref[pl.ds(start, KEY_TILE), pl.ds(HEAD_DIM, HEAD_DIM)]
        probability = jnp.exp(jnp.where(allowed_at(tile), scores_at(tile) - log_total, MASKED))
        grad_probs = lax.dot_general(
            grad_block, values, (((1,), (1,)), ((), ())), preferred_element_type=jnp.float32
        ).reshape(heads, local_rows, KEY_TILE)
        grad_scores = (
            (probability * (grad_probs - dots)).astype(jnp.bfloat16).reshape(rows, KEY_TILE)
        )
        probs_low = probability.astype(jnp.bfloat16).reshape(rows, KEY_TILE)
        key_part = (
            jnp.dot(grad_scores.T, query_block, preferred_element_type=jnp.float32) * scale_factor
        )
        value_part = jnp.dot(probs_low.T, grad_block, preferred_element_type=jnp.float32)
        dkv_ref[pl.ds(start, KEY_TILE), pl.ds(0, HEAD_DIM)] = key_part.astype(dkv_ref.dtype)
        dkv_ref[pl.ds(start, KEY_TILE), pl.ds(HEAD_DIM, HEAD_DIM)] = value_part.astype(
            dkv_ref.dtype
        )
        return query_now + jnp.dot(grad_scores, keys, preferred_element_type=jnp.float32)

    query_now = lax.fori_loop(0, tiles, gradients, jnp.zeros((rows, HEAD_DIM), jnp.float32))
    dq_ref[...] = query_now * scale_factor


def attention_backward(q2, g2, dots2, qpos2, qframe2, kv, kpos2, kframe2):
    rows = q2.shape[0]
    return pl.pallas_call(
        backward_kernel,
        out_shape=(
            jax.ShapeDtypeStruct((rows, HEAD_DIM), jnp.float32),
            jax.ShapeDtypeStruct(kv.shape, jnp.bfloat16),
        ),
        interpret=INTERPRET,
    )(q2, g2, dots2, qpos2, qframe2, kv, kpos2, kframe2)


def shards(
    query_vectors,
    key_vectors,
    value_vectors,
    grad_output,
    output_dots,
    frame_ids,
    visual_rows,
    shuffle_source,
    qkv_weight,
    projector_weight,
):
    ring_z = lax.axis_size("cz")
    ring_y = lax.axis_size("cy")
    position = lax.axis_index("cz") * ring_y + lax.axis_index("cy")
    local_rows = query_vectors.shape[1]
    scale_factor = 1.0 / math.sqrt(HEAD_DIM)
    query_heads = query_vectors[0].reshape(local_rows, GROUP, HEAD_DIM)
    grad_heads = grad_output[0].reshape(local_rows, GROUP, HEAD_DIM)
    corrections = output_dots[0]
    frame_line = frame_ids[0]
    seq_total = frame_line.shape[0]
    query_first = position * local_rows
    query_pos = query_first + jnp.arange(local_rows, dtype=jnp.int32)
    query_frames = lax.dynamic_slice_in_dim(frame_line, query_first, local_rows)

    own_pair = jnp.concatenate([key_vectors[0], value_vectors[0]], axis=1)
    all_pairs = lax.all_gather(
        lax.all_to_all(jnp.tile(own_pair, (ring_z, 1)), "cz", 0, 0, tiled=True),
        "cy",
        axis=0,
        tiled=True,
    )

    key_pos = (
        jnp.arange(seq_total, dtype=jnp.int32)
        .reshape(ring_z, ring_y, local_rows)
        .transpose(1, 0, 2)
        .reshape(seq_total)
    )
    key_frames = (
        frame_line.reshape(ring_z, ring_y, local_rows).transpose(1, 0, 2).reshape(seq_total)
    )
    rows = GROUP * local_rows
    q2 = query_heads.transpose(1, 0, 2).reshape(rows, HEAD_DIM)
    g2 = grad_heads.transpose(1, 0, 2).reshape(rows, HEAD_DIM)
    dots2 = corrections.reshape(rows, 1)
    qpos2 = query_pos.reshape(local_rows, 1)
    qframe2 = query_frames.reshape(local_rows, 1)
    tiles = seq_total // KEY_TILE
    dq2, partials = attention_backward(
        q2,
        g2,
        dots2,
        qpos2,
        qframe2,
        all_pairs,
        key_pos.reshape(tiles, KEY_TILE),
        key_frames.reshape(tiles, KEY_TILE),
    )
    grad_query = dq2.reshape(GROUP, local_rows, HEAD_DIM).transpose(1, 0, 2)
    stage_one = lax.psum_scatter(
        partials,
        "cy",
        scatter_dimension=0,
        tiled=True,
    )
    stage_two = lax.all_to_all(stage_one, "cz", 0, 0, tiled=True)
    summed_grads = (
        stage_two.astype(jnp.float32).reshape(ring_z, local_rows, stage_two.shape[1]).sum(0)
    )
    grad_keys_low = summed_grads[:, :HEAD_DIM].astype(jnp.bfloat16)
    grad_values_low = summed_grads[:, HEAD_DIM:].astype(jnp.bfloat16)
    grad_query_low = grad_query.astype(jnp.bfloat16).reshape(local_rows, GROUP * HEAD_DIM)
    visual_picks = visual_rows[0, 0]
    chosen = jnp.concatenate(
        [grad_query_low[visual_picks], grad_keys_low[visual_picks], grad_values_low[visual_picks]],
        axis=1,
    )
    everyone = lax.all_gather(chosen[None], ("section", "dp"), axis=0, tiled=True)
    groups = lax.axis_size("section")
    replicas = lax.axis_size("dp")
    half_rows = visual_picks.shape[0] // 2
    width_in = chosen.shape[1]
    arranged = (
        everyone.reshape(groups, replicas, 2, half_rows, width_in)
        .transpose(2, 1, 3, 0, 4)
        .reshape(2 * replicas * half_rows, groups * width_in)
    )
    visual_grad = jnp.dot(arranged, qkv_weight, preferred_element_type=jnp.float32).astype(
        jnp.bfloat16
    )
    pieces = lax.all_to_all(
        jnp.dot(visual_grad, projector_weight, preferred_element_type=jnp.float32).astype(
            jnp.bfloat16
        ),
        ("section", "dp"),
        0,
        0,
        tiled=True,
    )
    shuffled = pieces.astype(jnp.float32).reshape(groups * replicas, -1, pieces.shape[1]).sum(0)
    slot_rows = shuffled.reshape(half_rows * 4, projector_weight.shape[1] // 4)
    patches = slot_rows[shuffle_source[0, 0]].astype(jnp.bfloat16)
    return (grad_keys_low[None], grad_values_low[None], patches[None])


def solution(mesh):
    ctx_size = mesh.shape["ctx"]
    ring_y = 8 if ctx_size % 8 == 0 else 1
    split_mesh = jax.sharding.Mesh(
        mesh.devices.reshape(
            ctx_size // ring_y, ring_y, mesh.shape["section"], mesh.shape["dp"]
        ),
        ("cz", "cy", "section", "dp"),
    )
    ctx = ("cz", "cy")
    placed = (
        P("dp", ctx, "section"),
        P("dp", ctx, "section"),
        P("dp", ctx, "section"),
        P("dp", ctx, "section"),
        P("dp", "section", ctx),
        P("dp", None),
        P("dp", ctx, None),
        P("dp", ("cz", "cy", "section"), None),
        P(None, ("section", "dp")),
        P(("section", "dp"), None),
    )
    return jax.shard_map(
        shards,
        mesh=split_mesh,
        in_specs=placed,
        out_specs=(
            P("dp", ctx, "section"),
            P("dp", ctx, "section"),
            P("dp", ("cz", "cy", "section"), None),
        ),
        check_vma=False,
    )
```

```python
import math

import jax
import jax.numpy as jnp
from jax import lax
from jax.experimental import pallas as pl
from jax.experimental.pallas import tpu as pltpu
from jax.sharding import PartitionSpec as P

HEAD_DIM = 128
GROUP = 7


MASKED = -1e30
KEY_TILE = 2048
INTERPRET = False


def backward_kernel(
    q_ref, g_ref, dots_ref, qpos_ref, qframe_ref, kv_ref, kpos_ref, kframe_ref, dq_ref, dkv_ref
):
    rows = q_ref.shape[0]
    local_rows = qpos_ref.shape[0]
    heads = rows // local_rows
    tiles = kpos_ref.shape[0]
    scale_factor = 1.0 / math.sqrt(HEAD_DIM)
    query_block = q_ref[...]
    grad_block = g_ref[...]
    qpos = qpos_ref[...]
    qframe = qframe_ref[...]

    def allowed_at(tile):
        kpos = kpos_ref[pl.ds(tile, 1), :]
        kframe = kframe_ref[pl.ds(tile, 1), :]
        return ((kpos <= qpos) | (kframe == qframe))[None]

    def scores_at(tile):
        start = pl.multiple_of(tile * KEY_TILE, KEY_TILE)
        keys = kv_ref[pl.ds(start, KEY_TILE), pl.ds(0, HEAD_DIM)]
        scores = (
            lax.dot_general(
                query_block, keys, (((1,), (1,)), ((), ())), preferred_element_type=jnp.float32
            )
            * scale_factor
        )
        return scores.reshape(heads, local_rows, KEY_TILE)

    def statistics(tile, carried):
        running, summed = carried
        scores = jnp.where(allowed_at(tile), scores_at(tile), MASKED)
        newest = jnp.maximum(running, scores.max(axis=2, keepdims=True))
        summed = summed * jnp.exp(running - newest) + jnp.exp(scores - newest).sum(
            axis=2, keepdims=True
        )
        return (newest, summed)

    running, summed = lax.fori_loop(
        0,
        tiles,
        statistics,
        (
            jnp.full((heads, local_rows, 1), MASKED, jnp.float32),
            jnp.zeros((heads, local_rows, 1), jnp.float32),
        ),
    )
    log_total = running + jnp.log(summed)
    dots = dots_ref[...].reshape(heads, local_rows, 1)

    def gradients(tile, query_now):
        start = pl.multiple_of(tile * KEY_TILE, KEY_TILE)
        keys = kv_ref[pl.ds(start, KEY_TILE), pl.ds(0, HEAD_DIM)]
        values = kv_ref[pl.ds(start, KEY_TILE), pl.ds(HEAD_DIM, HEAD_DIM)]
        probability = jnp.exp(jnp.where(allowed_at(tile), scores_at(tile) - log_total, MASKED))
        grad_probs = lax.dot_general(
            grad_block, values, (((1,), (1,)), ((), ())), preferred_element_type=jnp.float32
        ).reshape(heads, local_rows, KEY_TILE)
        grad_scores = (
            (probability * (grad_probs - dots)).astype(jnp.bfloat16).reshape(rows, KEY_TILE)
        )
        probs_low = probability.astype(jnp.bfloat16).reshape(rows, KEY_TILE)
        key_part = (
            jnp.dot(grad_scores.T, query_block, preferred_element_type=jnp.float32) * scale_factor
        )
        value_part = jnp.dot(probs_low.T, grad_block, preferred_element_type=jnp.float32)
        dkv_ref[pl.ds(start, KEY_TILE), pl.ds(0, HEAD_DIM)] = key_part.astype(dkv_ref.dtype)
        dkv_ref[pl.ds(start, KEY_TILE), pl.ds(HEAD_DIM, HEAD_DIM)] = value_part.astype(
            dkv_ref.dtype
        )
        return query_now + jnp.dot(grad_scores, keys, preferred_element_type=jnp.float32)

    query_now = lax.fori_loop(0, tiles, gradients, jnp.zeros((rows, HEAD_DIM), jnp.float32))
    dq_ref[...] = query_now * scale_factor


def attention_backward(q2, g2, dots2, qpos2, qframe2, kv, kpos2, kframe2):
    rows = q2.shape[0]
    return pl.pallas_call(
        backward_kernel,
        out_shape=(
            jax.ShapeDtypeStruct((rows, HEAD_DIM), jnp.float32),
            jax.ShapeDtypeStruct(kv.shape, jnp.bfloat16),
        ),
        interpret=INTERPRET,
    )(q2, g2, dots2, qpos2, qframe2, kv, kpos2, kframe2)


def shards(
    query_vectors,
    key_vectors,
    value_vectors,
    grad_output,
    output_dots,
    frame_ids,
    visual_rows,
    shuffle_source,
    qkv_weight,
    projector_weight,
):
    ring_z = lax.axis_size("cz")
    ring_y = lax.axis_size("cy")
    position = lax.axis_index("cz") * ring_y + lax.axis_index("cy")
    local_rows = query_vectors.shape[1]
    scale_factor = 1.0 / math.sqrt(HEAD_DIM)
    query_heads = query_vectors[0].reshape(local_rows, GROUP, HEAD_DIM)
    grad_heads = grad_output[0].reshape(local_rows, GROUP, HEAD_DIM)
    corrections = output_dots[0]
    frame_line = frame_ids[0]
    seq_total = frame_line.shape[0]
    query_first = position * local_rows
    query_pos = query_first + jnp.arange(local_rows, dtype=jnp.int32)
    query_frames = lax.dynamic_slice_in_dim(frame_line, query_first, local_rows)

    own_pair = jnp.concatenate([key_vectors[0], value_vectors[0]], axis=1)
    all_pairs = lax.all_gather(
        lax.all_to_all(jnp.tile(own_pair, (ring_z, 1)), "cz", 0, 0, tiled=True),
        "cy",
        axis=0,
        tiled=True,
    )

    key_pos = (
        jnp.arange(seq_total, dtype=jnp.int32)
        .reshape(ring_z, ring_y, local_rows)
        .transpose(1, 0, 2)
        .reshape(seq_total)
    )
    key_frames = (
        frame_line.reshape(ring_z, ring_y, local_rows).transpose(1, 0, 2).reshape(seq_total)
    )
    rows = GROUP * local_rows
    q2 = query_heads.transpose(1, 0, 2).reshape(rows, HEAD_DIM)
    g2 = grad_heads.transpose(1, 0, 2).reshape(rows, HEAD_DIM)
    dots2 = corrections.reshape(rows, 1)
    qpos2 = query_pos.reshape(local_rows, 1)
    qframe2 = query_frames.reshape(local_rows, 1)
    tiles = seq_total // KEY_TILE
    dq2, partials = attention_backward(
        q2,
        g2,
        dots2,
        qpos2,
        qframe2,
        all_pairs,
        key_pos.reshape(tiles, KEY_TILE),
        key_frames.reshape(tiles, KEY_TILE),
    )
    grad_query = dq2.reshape(GROUP, local_rows, HEAD_DIM).transpose(1, 0, 2)
    received = lax.all_to_all(partials, "cy", 0, 0, tiled=True)
    stage_one = (
        received.astype(jnp.float32)
        .reshape(ring_y, seq_total // ring_y, received.shape[1])
        .sum(0)
        .astype(jnp.bfloat16)
    )
    stage_two = lax.all_to_all(stage_one, "cz", 0, 0, tiled=True)
    summed_grads = (
        stage_two.astype(jnp.float32).reshape(ring_z, local_rows, stage_two.shape[1]).sum(0)
    )
    grad_keys_low = summed_grads[:, :HEAD_DIM].astype(jnp.bfloat16)
    grad_values_low = summed_grads[:, HEAD_DIM:].astype(jnp.bfloat16)
    grad_query_low = grad_query.astype(jnp.bfloat16).reshape(local_rows, GROUP * HEAD_DIM)
    visual_picks = visual_rows[0, 0]
    chosen = jnp.concatenate(
        [grad_query_low[visual_picks], grad_keys_low[visual_picks], grad_values_low[visual_picks]],
        axis=1,
    )
    everyone = lax.all_gather(chosen[None], ("section", "dp"), axis=0, tiled=True)
    groups = lax.axis_size("section")
    replicas = lax.axis_size("dp")
    half_rows = visual_picks.shape[0] // 2
    width_in = chosen.shape[1]
    arranged = (
        everyone.reshape(groups, replicas, 2, half_rows, width_in)
        .transpose(2, 1, 3, 0, 4)
        .reshape(2 * replicas * half_rows, groups * width_in)
    )
    visual_grad = jnp.dot(arranged, qkv_weight, preferred_element_type=jnp.float32).astype(
        jnp.bfloat16
    )
    pieces = lax.all_to_all(
        jnp.dot(visual_grad, projector_weight, preferred_element_type=jnp.float32).astype(
            jnp.bfloat16
        ),
        ("section", "dp"),
        0,
        0,
        tiled=True,
    )
    shuffled = pieces.astype(jnp.float32).reshape(groups * replicas, -1, pieces.shape[1]).sum(0)
    slot_rows = shuffled.reshape(half_rows * 4, projector_weight.shape[1] // 4)
    patches = slot_rows[shuffle_source[0, 0]].astype(jnp.bfloat16)
    return (grad_keys_low[None], grad_values_low[None], patches[None])


def solution(mesh):
    ctx_size = mesh.shape["ctx"]
    ring_y = 8 if ctx_size % 8 == 0 else 1
    split_mesh = jax.sharding.Mesh(
        mesh.devices.reshape(
            ctx_size // ring_y, ring_y, mesh.shape["section"], mesh.shape["dp"]
        ),
        ("cz", "cy", "section", "dp"),
    )
    ctx = ("cz", "cy")
    placed = (
        P("dp", ctx, "section"),
        P("dp", ctx, "section"),
        P("dp", ctx, "section"),
        P("dp", ctx, "section"),
        P("dp", "section", ctx),
        P("dp", None),
        P("dp", ctx, None),
        P("dp", ("cz", "cy", "section"), None),
        P(None, ("section", "dp")),
        P(("section", "dp"), None),
    )
    return jax.shard_map(
        shards,
        mesh=split_mesh,
        in_specs=placed,
        out_specs=(
            P("dp", ctx, "section"),
            P("dp", ctx, "section"),
            P("dp", ("cz", "cy", "section"), None),
        ),
        check_vma=False,
    )
```

```python
import math

import jax
import jax.numpy as jnp
from jax import lax
from jax.experimental import pallas as pl
from jax.experimental.pallas import tpu as pltpu
from jax.sharding import PartitionSpec as P

HEAD_DIM = 128
GROUP = 7


MASKED = -1e30
KEY_TILE = 2048
INTERPRET = False


def backward_kernel(
    q_ref, g_ref, dots_ref, qpos_ref, qframe_ref, kv_ref, kpos_ref, kframe_ref, dq_ref, dkv_ref
):
    rows = q_ref.shape[0]
    local_rows = qpos_ref.shape[0]
    heads = rows // local_rows
    tiles = kpos_ref.shape[0]
    scale_factor = 1.0 / math.sqrt(HEAD_DIM)
    query_block = q_ref[...]
    grad_block = g_ref[...]
    qpos = qpos_ref[...]
    qframe = qframe_ref[...]

    def allowed_at(tile):
        kpos = kpos_ref[pl.ds(tile, 1), :]
        kframe = kframe_ref[pl.ds(tile, 1), :]
        return ((kpos <= qpos) | (kframe == qframe))[None]

    def scores_at(tile):
        start = pl.multiple_of(tile * KEY_TILE, KEY_TILE)
        keys = kv_ref[pl.ds(start, KEY_TILE), pl.ds(0, HEAD_DIM)]
        scores = (
            lax.dot_general(
                query_block, keys, (((1,), (1,)), ((), ())), preferred_element_type=jnp.float32
            )
            * scale_factor
        )
        return scores.reshape(heads, local_rows, KEY_TILE)

    def statistics(tile, carried):
        running, summed = carried
        scores = jnp.where(allowed_at(tile), scores_at(tile), MASKED)
        newest = jnp.maximum(running, scores.max(axis=2, keepdims=True))
        summed = summed * jnp.exp(running - newest) + jnp.exp(scores - newest).sum(
            axis=2, keepdims=True
        )
        return (newest, summed)

    running, summed = lax.fori_loop(
        0,
        tiles,
        statistics,
        (
            jnp.full((heads, local_rows, 1), MASKED, jnp.float32),
            jnp.zeros((heads, local_rows, 1), jnp.float32),
        ),
    )
    log_total = running + jnp.log(summed)
    dots = dots_ref[...].reshape(heads, local_rows, 1)

    def gradients(tile, query_now):
        start = pl.multiple_of(tile * KEY_TILE, KEY_TILE)
        keys = kv_ref[pl.ds(start, KEY_TILE), pl.ds(0, HEAD_DIM)]
        values = kv_ref[pl.ds(start, KEY_TILE), pl.ds(HEAD_DIM, HEAD_DIM)]
        probability = jnp.exp(jnp.where(allowed_at(tile), scores_at(tile) - log_total, MASKED))
        grad_probs = lax.dot_general(
            grad_block, values, (((1,), (1,)), ((), ())), preferred_element_type=jnp.float32
        ).reshape(heads, local_rows, KEY_TILE)
        grad_scores = (
            (probability * (grad_probs - dots)).astype(jnp.bfloat16).reshape(rows, KEY_TILE)
        )
        probs_low = probability.astype(jnp.bfloat16).reshape(rows, KEY_TILE)
        key_part = (
            jnp.dot(grad_scores.T, query_block, preferred_element_type=jnp.float32) * scale_factor
        )
        value_part = jnp.dot(probs_low.T, grad_block, preferred_element_type=jnp.float32)
        dkv_ref[pl.ds(start, KEY_TILE), pl.ds(0, HEAD_DIM)] = key_part.astype(dkv_ref.dtype)
        dkv_ref[pl.ds(start, KEY_TILE), pl.ds(HEAD_DIM, HEAD_DIM)] = value_part.astype(
            dkv_ref.dtype
        )
        return query_now + jnp.dot(grad_scores, keys, preferred_element_type=jnp.float32)

    query_now = lax.fori_loop(0, tiles, gradients, jnp.zeros((rows, HEAD_DIM), jnp.float32))
    dq_ref[...] = query_now * scale_factor


def attention_backward(q2, g2, dots2, qpos2, qframe2, kv, kpos2, kframe2):
    rows = q2.shape[0]
    return pl.pallas_call(
        backward_kernel,
        out_shape=(
            jax.ShapeDtypeStruct((rows, HEAD_DIM), jnp.float32),
            jax.ShapeDtypeStruct(kv.shape, jnp.bfloat16),
        ),
        interpret=INTERPRET,
    )(q2, g2, dots2, qpos2, qframe2, kv, kpos2, kframe2)


def shards(
    query_vectors,
    key_vectors,
    value_vectors,
    grad_output,
    output_dots,
    frame_ids,
    visual_rows,
    shuffle_source,
    qkv_weight,
    projector_weight,
):
    ring_z = lax.axis_size("cz")
    ring_y = lax.axis_size("cy")
    position = lax.axis_index("cz") * ring_y + lax.axis_index("cy")
    local_rows = query_vectors.shape[1]
    scale_factor = 1.0 / math.sqrt(HEAD_DIM)
    query_heads = query_vectors[0].reshape(local_rows, GROUP, HEAD_DIM)
    grad_heads = grad_output[0].reshape(local_rows, GROUP, HEAD_DIM)
    corrections = output_dots[0]
    frame_line = frame_ids[0]
    seq_total = frame_line.shape[0]
    query_first = position * local_rows
    query_pos = query_first + jnp.arange(local_rows, dtype=jnp.int32)
    query_frames = lax.dynamic_slice_in_dim(frame_line, query_first, local_rows)

    own_pair = jnp.concatenate([key_vectors[0], value_vectors[0]], axis=1)
    all_pairs = lax.all_gather(
        lax.all_to_all(jnp.tile(own_pair, (ring_y, 1)), "cy", 0, 0, tiled=True),
        "cz",
        axis=0,
        tiled=True,
    )

    key_pos = jnp.arange(seq_total, dtype=jnp.int32)
    key_frames = frame_line
    rows = GROUP * local_rows
    q2 = query_heads.transpose(1, 0, 2).reshape(rows, HEAD_DIM)
    g2 = grad_heads.transpose(1, 0, 2).reshape(rows, HEAD_DIM)
    dots2 = corrections.reshape(rows, 1)
    qpos2 = query_pos.reshape(local_rows, 1)
    qframe2 = query_frames.reshape(local_rows, 1)
    tiles = seq_total // KEY_TILE
    dq2, partials = attention_backward(
        q2,
        g2,
        dots2,
        qpos2,
        qframe2,
        all_pairs,
        key_pos.reshape(tiles, KEY_TILE),
        key_frames.reshape(tiles, KEY_TILE),
    )
    grad_query = dq2.reshape(GROUP, local_rows, HEAD_DIM).transpose(1, 0, 2)
    stage_one = lax.psum_scatter(
        partials,
        "cz",
        scatter_dimension=0,
        tiled=True,
    )
    stage_two = lax.all_to_all(stage_one, "cy", 0, 0, tiled=True)
    summed_grads = (
        stage_two.astype(jnp.float32).reshape(ring_y, local_rows, stage_two.shape[1]).sum(0)
    )
    grad_keys_low = summed_grads[:, :HEAD_DIM].astype(jnp.bfloat16)
    grad_values_low = summed_grads[:, HEAD_DIM:].astype(jnp.bfloat16)
    grad_query_low = grad_query.astype(jnp.bfloat16).reshape(local_rows, GROUP * HEAD_DIM)
    visual_picks = visual_rows[0, 0]
    chosen = jnp.concatenate(
        [grad_query_low[visual_picks], grad_keys_low[visual_picks], grad_values_low[visual_picks]],
        axis=1,
    )
    everyone = lax.all_gather(chosen[None], ("section", "dp"), axis=0, tiled=True)
    groups = lax.axis_size("section")
    replicas = lax.axis_size("dp")
    half_rows = visual_picks.shape[0] // 2
    width_in = chosen.shape[1]
    arranged = (
        everyone.reshape(groups, replicas, 2, half_rows, width_in)
        .transpose(2, 1, 3, 0, 4)
        .reshape(2 * replicas * half_rows, groups * width_in)
    )
    visual_grad = jnp.dot(arranged, qkv_weight, preferred_element_type=jnp.float32).astype(
        jnp.bfloat16
    )
    pieces = lax.all_to_all(
        jnp.dot(visual_grad, projector_weight, preferred_element_type=jnp.float32).astype(
            jnp.bfloat16
        ),
        ("section", "dp"),
        0,
        0,
        tiled=True,
    )
    shuffled = pieces.astype(jnp.float32).reshape(groups * replicas, -1, pieces.shape[1]).sum(0)
    slot_rows = shuffled.reshape(half_rows * 4, projector_weight.shape[1] // 4)
    patches = slot_rows[shuffle_source[0, 0]].astype(jnp.bfloat16)
    return (grad_keys_low[None], grad_values_low[None], patches[None])


def solution(mesh):
    ctx_size = mesh.shape["ctx"]
    ring_y = 8 if ctx_size % 8 == 0 else 1
    split_mesh = jax.sharding.Mesh(
        mesh.devices.reshape(
            ctx_size // ring_y, ring_y, mesh.shape["section"], mesh.shape["dp"]
        ),
        ("cz", "cy", "section", "dp"),
    )
    ctx = ("cz", "cy")
    placed = (
        P("dp", ctx, "section"),
        P("dp", ctx, "section"),
        P("dp", ctx, "section"),
        P("dp", ctx, "section"),
        P("dp", "section", ctx),
        P("dp", None),
        P("dp", ctx, None),
        P("dp", ("cz", "cy", "section"), None),
        P(None, ("section", "dp")),
        P(("section", "dp"), None),
    )
    return jax.shard_map(
        shards,
        mesh=split_mesh,
        in_specs=placed,
        out_specs=(
            P("dp", ctx, "section"),
            P("dp", ctx, "section"),
            P("dp", ("cz", "cy", "section"), None),
        ),
        check_vma=False,
    )
```

```python
import math

import jax
import jax.numpy as jnp
from jax import lax
from jax.experimental import pallas as pl
from jax.experimental.pallas import tpu as pltpu
from jax.sharding import PartitionSpec as P

HEAD_DIM = 128
GROUP = 7


MASKED = -1e30
KEY_TILE = 2048
INTERPRET = False


def backward_kernel(
    q_ref, g_ref, dots_ref, qpos_ref, qframe_ref, kv_ref, kpos_ref, kframe_ref, dq_ref, dkv_ref
):
    rows = q_ref.shape[0]
    local_rows = qpos_ref.shape[0]
    heads = rows // local_rows
    tiles = kpos_ref.shape[0]
    scale_factor = 1.0 / math.sqrt(HEAD_DIM)
    query_block = q_ref[...]
    grad_block = g_ref[...]
    qpos = qpos_ref[...]
    qframe = qframe_ref[...]

    def allowed_at(tile):
        kpos = kpos_ref[pl.ds(tile, 1), :]
        kframe = kframe_ref[pl.ds(tile, 1), :]
        return ((kpos <= qpos) | (kframe == qframe))[None]

    def scores_at(tile):
        start = pl.multiple_of(tile * KEY_TILE, KEY_TILE)
        keys = kv_ref[pl.ds(start, KEY_TILE), pl.ds(0, HEAD_DIM)]
        scores = (
            lax.dot_general(
                query_block, keys, (((1,), (1,)), ((), ())), preferred_element_type=jnp.float32
            )
            * scale_factor
        )
        return scores.reshape(heads, local_rows, KEY_TILE)

    def statistics(tile, carried):
        running, summed = carried
        scores = jnp.where(allowed_at(tile), scores_at(tile), MASKED)
        newest = jnp.maximum(running, scores.max(axis=2, keepdims=True))
        summed = summed * jnp.exp(running - newest) + jnp.exp(scores - newest).sum(
            axis=2, keepdims=True
        )
        return (newest, summed)

    running, summed = lax.fori_loop(
        0,
        tiles,
        statistics,
        (
            jnp.full((heads, local_rows, 1), MASKED, jnp.float32),
            jnp.zeros((heads, local_rows, 1), jnp.float32),
        ),
        unroll=True,
    )
    log_total = running + jnp.log(summed)
    dots = dots_ref[...].reshape(heads, local_rows, 1)

    def gradients(tile, query_now):
        start = pl.multiple_of(tile * KEY_TILE, KEY_TILE)
        keys = kv_ref[pl.ds(start, KEY_TILE), pl.ds(0, HEAD_DIM)]
        values = kv_ref[pl.ds(start, KEY_TILE), pl.ds(HEAD_DIM, HEAD_DIM)]
        probability = jnp.exp(jnp.where(allowed_at(tile), scores_at(tile) - log_total, MASKED))
        grad_probs = lax.dot_general(
            grad_block, values, (((1,), (1,)), ((), ())), preferred_element_type=jnp.float32
        ).reshape(heads, local_rows, KEY_TILE)
        grad_scores = (
            (probability * (grad_probs - dots)).astype(jnp.bfloat16).reshape(rows, KEY_TILE)
        )
        probs_low = probability.astype(jnp.bfloat16).reshape(rows, KEY_TILE)
        key_part = (
            jnp.dot(grad_scores.T, query_block, preferred_element_type=jnp.float32) * scale_factor
        )
        value_part = jnp.dot(probs_low.T, grad_block, preferred_element_type=jnp.float32)
        dkv_ref[pl.ds(start, KEY_TILE), pl.ds(0, HEAD_DIM)] = key_part.astype(dkv_ref.dtype)
        dkv_ref[pl.ds(start, KEY_TILE), pl.ds(HEAD_DIM, HEAD_DIM)] = value_part.astype(
            dkv_ref.dtype
        )
        return query_now + jnp.dot(grad_scores, keys, preferred_element_type=jnp.float32)

    query_now = lax.fori_loop(0, tiles, gradients, jnp.zeros((rows, HEAD_DIM), jnp.float32))
    dq_ref[...] = query_now * scale_factor


def attention_backward(q2, g2, dots2, qpos2, qframe2, kv, kpos2, kframe2):
    rows = q2.shape[0]
    return pl.pallas_call(
        backward_kernel,
        out_shape=(
            jax.ShapeDtypeStruct((rows, HEAD_DIM), jnp.float32),
            jax.ShapeDtypeStruct(kv.shape, jnp.bfloat16),
        ),
        interpret=INTERPRET,
    )(q2, g2, dots2, qpos2, qframe2, kv, kpos2, kframe2)


def shards(
    query_vectors,
    key_vectors,
    value_vectors,
    grad_output,
    output_dots,
    frame_ids,
    visual_rows,
    shuffle_source,
    qkv_weight,
    projector_weight,
):
    ring_z = lax.axis_size("cz")
    ring_y = lax.axis_size("cy")
    position = lax.axis_index("cz") * ring_y + lax.axis_index("cy")
    local_rows = query_vectors.shape[1]
    scale_factor = 1.0 / math.sqrt(HEAD_DIM)
    query_heads = query_vectors[0].reshape(local_rows, GROUP, HEAD_DIM)
    grad_heads = grad_output[0].reshape(local_rows, GROUP, HEAD_DIM)
    corrections = output_dots[0]
    frame_line = frame_ids[0]
    seq_total = frame_line.shape[0]
    query_first = position * local_rows
    query_pos = query_first + jnp.arange(local_rows, dtype=jnp.int32)
    query_frames = lax.dynamic_slice_in_dim(frame_line, query_first, local_rows)

    own_pair = jnp.concatenate([key_vectors[0], value_vectors[0]], axis=1)
    all_pairs = lax.all_gather(
        lax.all_to_all(jnp.tile(own_pair, (ring_z, 1)), "cz", 0, 0, tiled=True),
        "cy",
        axis=0,
        tiled=True,
    )

    key_pos = (
        jnp.arange(seq_total, dtype=jnp.int32)
        .reshape(ring_z, ring_y, local_rows)
        .transpose(1, 0, 2)
        .reshape(seq_total)
    )
    key_frames = (
        frame_line.reshape(ring_z, ring_y, local_rows).transpose(1, 0, 2).reshape(seq_total)
    )
    rows = GROUP * local_rows
    q2 = query_heads.transpose(1, 0, 2).reshape(rows, HEAD_DIM)
    g2 = grad_heads.transpose(1, 0, 2).reshape(rows, HEAD_DIM)
    dots2 = corrections.reshape(rows, 1)
    qpos2 = query_pos.reshape(local_rows, 1)
    qframe2 = query_frames.reshape(local_rows, 1)
    tiles = seq_total // KEY_TILE
    dq2, partials = attention_backward(
        q2,
        g2,
        dots2,
        qpos2,
        qframe2,
        all_pairs,
        key_pos.reshape(tiles, KEY_TILE),
        key_frames.reshape(tiles, KEY_TILE),
    )
    grad_query = dq2.reshape(GROUP, local_rows, HEAD_DIM).transpose(1, 0, 2)
    stage_one = lax.psum_scatter(
        partials,
        "cy",
        scatter_dimension=0,
        tiled=True,
    )
    stage_two = lax.all_to_all(stage_one, "cz", 0, 0, tiled=True)
    summed_grads = (
        stage_two.astype(jnp.float32).reshape(ring_z, local_rows, stage_two.shape[1]).sum(0)
    )
    grad_keys_low = summed_grads[:, :HEAD_DIM].astype(jnp.bfloat16)
    grad_values_low = summed_grads[:, HEAD_DIM:].astype(jnp.bfloat16)
    grad_query_low = grad_query.astype(jnp.bfloat16).reshape(local_rows, GROUP * HEAD_DIM)
    visual_picks = visual_rows[0, 0]
    chosen = jnp.concatenate(
        [grad_query_low[visual_picks], grad_keys_low[visual_picks], grad_values_low[visual_picks]],
        axis=1,
    )
    everyone = lax.all_gather(chosen[None], ("section", "dp"), axis=0, tiled=True)
    groups = lax.axis_size("section")
    replicas = lax.axis_size("dp")
    half_rows = visual_picks.shape[0] // 2
    width_in = chosen.shape[1]
    arranged = (
        everyone.reshape(groups, replicas, 2, half_rows, width_in)
        .transpose(2, 1, 3, 0, 4)
        .reshape(2 * replicas * half_rows, groups * width_in)
    )
    visual_grad = jnp.dot(arranged, qkv_weight, preferred_element_type=jnp.float32).astype(
        jnp.bfloat16
    )
    pieces = lax.all_to_all(
        jnp.dot(visual_grad, projector_weight, preferred_element_type=jnp.float32).astype(
            jnp.bfloat16
        ),
        ("section", "dp"),
        0,
        0,
        tiled=True,
    )
    shuffled = pieces.astype(jnp.float32).reshape(groups * replicas, -1, pieces.shape[1]).sum(0)
    slot_rows = shuffled.reshape(half_rows * 4, projector_weight.shape[1] // 4)
    patches = slot_rows[shuffle_source[0, 0]].astype(jnp.bfloat16)
    return (grad_keys_low[None], grad_values_low[None], patches[None])


def solution(mesh):
    ctx_size = mesh.shape["ctx"]
    ring_y = 8 if ctx_size % 8 == 0 else 1
    split_mesh = jax.sharding.Mesh(
        mesh.devices.reshape(
            ctx_size // ring_y, ring_y, mesh.shape["section"], mesh.shape["dp"]
        ),
        ("cz", "cy", "section", "dp"),
    )
    ctx = ("cz", "cy")
    placed = (
        P("dp", ctx, "section"),
        P("dp", ctx, "section"),
        P("dp", ctx, "section"),
        P("dp", ctx, "section"),
        P("dp", "section", ctx),
        P("dp", None),
        P("dp", ctx, None),
        P("dp", ("cz", "cy", "section"), None),
        P(None, ("section", "dp")),
        P(("section", "dp"), None),
    )
    return jax.shard_map(
        shards,
        mesh=split_mesh,
        in_specs=placed,
        out_specs=(
            P("dp", ctx, "section"),
            P("dp", ctx, "section"),
            P("dp", ("cz", "cy", "section"), None),
        ),
        check_vma=False,
    )
```
